512 devices in a mesh: patch: 128 (over x, y, z_lo), head: 4 (over z_hi, core).
Axes of the slice: x: 4, y: 4, z: 16 (z_hi: 2, z_lo: 8; z = z_hi * 8 + z_lo), core: 2. Of those that a mesh axis runs over, the one named last changes fastest.
Arguments:
- x_tokens: bfloat16 [4096, 1536], P(('patch', 'head')), may hold values from -6 to 6
- shift: float32 [1536], replicated, may hold values from -3 to 3
- scale_mod: float32 [1536], replicated, may hold values from -3 to 3
- gate: float32 [1536], replicated, may hold values from -4 to 4
- w_qkv: bfloat16 [3, 1536, 1536], P(None, None, 'head'), may hold values from -0.2806707 to 0.2806707, as said below
- w_out: bfloat16 [1536, 1536], P('head'), may hold values from -0.15625 to 0.15625
- gain_q: float32 [1536], P('head'), may hold values from 0.1 to 1.9
- gain_k: float32 [1536], P('head'), may hold values from 1 to 3
- stale_kv: bfloat16 [2, 4096, 1536], P(None, 'patch', 'head'), may hold values from -60 to 60
Outputs:
- update: bfloat16 [4096, 1536], P(('patch', 'head'))
- fresh_kv: bfloat16 [2, 4096, 1536], P(None, 'patch', 'head')
The draws below stay inside these ranges and needn't reach their ends.
Inputs may be any that keep to these rules, and one draw needn't show every extreme that they name: `w_qkv`: projection weights of mean zero, of order 1536 ** -0.5.
All inputs are finite; a program needn't handle non-finite values.
Results may differ from the reference program's by a relative error of at most 0.01555.
The reference program's roundings to bfloat16 on the way count: a program that leaves them out, or rounds other values in their place, can miss the bound.
Values may be sent and summed in bfloat16 or wider, within the bound.
No kernel may reach another device: no remote copies, remote signals or barrier semaphores. Data moves between devices by JAX's collectives and lax.ppermute only.
A program may use at most 64 MiB of HBM per device.

```python
import math
import jax
import jax.numpy as jnp
from jax import lax

D = 1536
HEADS = 12
HD = 128
SLAB = 32
TOKENS = 4096
N_PATCH = 128


def draw_w_qkv(key, part):
    base = jnp.clip(jax.random.normal(key, (3, D, D), jnp.float32), -6.0, 6.0)
    head_ids = (jnp.arange(D) // HD).astype(jnp.float32)
    factor = 0.6 * 3.0 ** (head_ids / max(HEADS - 1, 1))
    return (base * factor * D ** (-0.5)).astype(jnp.bfloat16)


def draw_stale_kv(key, part):
    key_part = jax.random.fold_in(key, 11)
    value_part = jax.random.fold_in(key, 23)
    keys = 2.0 * jnp.clip(jax.random.normal(key_part, (1, TOKENS, D), jnp.float32), -6.0, 6.0)
    values = jnp.clip(jax.random.normal(value_part, (1, TOKENS, D), jnp.float32), -6.0, 6.0)
    return jnp.concatenate([keys, values], axis=0).astype(jnp.bfloat16)


def steps_of(key, extent, cuts, smallest, high):
    def one(position, shards_of):
        heights = jax.random.uniform(jax.random.fold_in(jax.random.fold_in(key, 6), position), (shards_of,), jnp.float32, smallest / len(cuts), high / len(cuts))
        return jnp.repeat(jnp.exp(heights), extent[position] // shards_of).reshape((-1,) + (1,) * (len(extent) - position - 1))

    loudness = one(*cuts[0])
    for cut in cuts[1:]:
        loudness = loudness * one(*cut)
    return loudness


def bell_draw(rng, dims, deviation, limit, shards=(), held_as=jnp.bfloat16):
    entries = deviation * jax.random.normal(rng, dims, jnp.float32)
    if shards:
        entries = entries * steps_of(rng, dims, shards, -0.22, 0.18)
    return jnp.clip(entries, -limit, limit).astype(held_as)


def setup_inputs(seed: int = 0) -> dict:
    key_of = jax.random.split(jax.random.key(seed), 10)
    x_tokens = bell_draw(key_of[0], (TOKENS, D), 1.0, 6.0, ((0, 512),))
    shift = bell_draw(key_of[1], (D,), 0.5, 3.0, (), jnp.float32)
    scale_mod = bell_draw(key_of[2], (D,), 0.5, 3.0, (), jnp.float32)
    gate = bell_draw(key_of[3], (D,), 1.0, 4.0, (), jnp.float32)
    w_qkv = draw_w_qkv(jax.random.fold_in(key_of[9], 71), 0)
    w_out = bell_draw(key_of[5], (D, D), D ** -0.5, 0.15625, ((0, 4),))
    gain_q = jnp.clip(1.0 + 0.18 * jax.random.normal(key_of[6], (D,), jnp.float32), 0.1, 1.9)
    gain_k = jnp.clip(jnp.exp(math.log(3.0) - 1.0986123 * jax.random.uniform(key_of[7], (D,), jnp.float32) ** steps_of(key_of[7], (D,), ((0, 4),), -0.2, 0.2)), 1.0, 3.0)
    stale_kv = draw_stale_kv(jax.random.fold_in(key_of[9], 71), 0)
    return {"x_tokens": x_tokens, "shift": shift, "scale_mod": scale_mod, "gate": gate, "w_qkv": w_qkv, "w_out": w_out, "gain_q": gain_q, "gain_k": gain_k, "stale_kv": stale_kv}


def modulate(x_tokens, shift, scale_mod):
    values_f = x_tokens.astype(jnp.float32)
    center = lax.optimization_barrier(jnp.mean(values_f, axis=-1, keepdims=True))
    spread = lax.optimization_barrier(jnp.mean((values_f - center) * (values_f - center), axis=-1, keepdims=True))
    return ((values_f - center) * lax.rsqrt(spread + 1e-06) * (1.0 + scale_mod) + shift).astype(jnp.bfloat16)

def reference(x_tokens, shift, scale_mod, gate, w_qkv, w_out, gain_q, gain_k, stale_kv):
    normed = modulate(x_tokens, shift, scale_mod)
    q_raw = jnp.dot(normed, w_qkv[0], preferred_element_type=jnp.float32)
    k_raw = jnp.dot(normed, w_qkv[1], preferred_element_type=jnp.float32)
    values = jnp.dot(normed, w_qkv[2], preferred_element_type=jnp.float32).astype(jnp.bfloat16)
    queries = (q_raw * lax.rsqrt(lax.optimization_barrier(jnp.mean(q_raw * q_raw, axis=-1, keepdims=True)) + 1e-06) * gain_q).astype(jnp.bfloat16)
    keys = (k_raw * lax.rsqrt(lax.optimization_barrier(jnp.mean(k_raw * k_raw, axis=-1, keepdims=True)) + 1e-06) * gain_k).astype(jnp.bfloat16)
    fresh_kv = jnp.stack([keys, values])
    query_slabs = queries.reshape(N_PATCH, SLAB, HEADS, HD)
    fresh_k = keys.reshape(N_PATCH, SLAB, HEADS, HD)
    fresh_v = values.reshape(N_PATCH, SLAB, HEADS, HD)
    stale_k = stale_kv[0].reshape(N_PATCH, SLAB, HEADS, HD)
    stale_v = stale_kv[1].reshape(N_PATCH, SLAB, HEADS, HD)
    block_ids = jnp.arange(N_PATCH, dtype=jnp.int32)

    def one_slab(item):
        index, query_block = item
        pick = (block_ids == index)[:, None, None, None]
        key_blocks = jnp.where(pick, fresh_k, stale_k).astype(jnp.float32)
        value_blocks = jnp.where(pick, fresh_v, stale_v).astype(jnp.float32)
        scores = jnp.einsum('qhd,bkhd->bhqk', query_block.astype(jnp.float32), key_blocks) / math.sqrt(HD)
        block_max = lax.optimization_barrier(jnp.max(scores, axis=-1))
        expo = jnp.exp(scores - block_max[..., None])
        totals = lax.optimization_barrier(jnp.sum(expo, axis=-1))
        weights = expo.astype(jnp.bfloat16).astype(jnp.float32)
        partial_out = jnp.einsum('bhqk,bkhd->bhqd', weights, value_blocks)
        top = lax.optimization_barrier(jnp.max(block_max, axis=0))
        factor = jnp.exp(block_max - top)
        numer = lax.optimization_barrier(jnp.sum(factor[..., None] * partial_out, axis=0))
        denom = lax.optimization_barrier(jnp.sum(factor * totals, axis=0))
        result = numer / denom[..., None]
        return jnp.transpose(result, (1, 0, 2)).reshape(SLAB, HEADS * HD).astype(jnp.bfloat16)
    attn = lax.map(one_slab, (block_ids, query_slabs)).reshape(TOKENS, D)
    projected = jnp.dot(attn, w_out, preferred_element_type=jnp.float32)
    update = (projected * gate).astype(jnp.bfloat16)
    return (update, fresh_kv)
```

```python
import math

import jax
import jax.numpy as jnp
from jax import lax
from jax.sharding import PartitionSpec as P

HD = 128


def modulate(x_tokens, shift, scale_mod):
    values_f = x_tokens.astype(jnp.float32)
    center = jnp.mean(values_f, axis=-1, keepdims=True)
    spread = jnp.mean((values_f - center) * (values_f - center), axis=-1, keepdims=True)
    return ((values_f - center) * lax.rsqrt(spread + 1e-06) * (1.0 + scale_mod) + shift).astype(
        jnp.bfloat16
    )


def per_device(x_tokens, shift, scale_mod, gate, w_qkv, w_out, gain_q, gain_k, stale_kv):
    normed = modulate(x_tokens, shift, scale_mod)
    width = w_qkv.shape[1]
    raw = jnp.einsum(
        "nd,cde->cne",
        lax.all_gather(normed, "head", axis=0, tiled=True),
        w_qkv,
        preferred_element_type=jnp.float32,
    )
    squares = jnp.sum(raw[:2] * raw[:2], axis=2)
    squares = lax.psum(squares, "head")
    inverse = lax.rsqrt(squares / width + 1e-06)
    queries = (raw[0] * inverse[0][:, None] * gain_q).astype(jnp.bfloat16)
    keys = (raw[1] * inverse[1][:, None] * gain_k).astype(jnp.bfloat16)
    values = raw[2].astype(jnp.bfloat16)
    fresh_kv = jnp.stack([keys, values])
    slab = queries.shape[0]
    local_heads = queries.shape[1] // HD
    query_heads = queries.reshape(slab, local_heads, HD)
    fresh_blocks = fresh_kv.reshape(2, 1, slab, local_heads, HD)
    own = lax.axis_index(PATCH)
    gathered = lax.all_gather(stale_kv, PATCH[-1], axis=1, tiled=True)
    if len(PATCH) > 1:
        gathered = lax.all_gather(gathered, PATCH[:-1], axis=1, tiled=True)
    count = gathered.shape[1] // slab
    blocks = gathered.reshape(2, count, slab, local_heads, HD)
    block_ids = 0 // slab + jnp.arange(count, dtype=jnp.int32)
    pick = (block_ids == own)[None, :, None, None, None]
    blocks = jnp.where(pick, fresh_blocks, blocks)
    scores = jnp.einsum(
        "qhd,bkhd->bhqk", query_heads, blocks[0], preferred_element_type=jnp.float32
    ) / math.sqrt(HD)
    block_max = jnp.max(scores, axis=-1)
    expo = jnp.exp(scores - block_max[..., None])
    totals = jnp.sum(expo, axis=-1)
    partial_out = jnp.einsum(
        "bhqk,bkhd->bhqd", expo.astype(jnp.bfloat16), blocks[1], preferred_element_type=jnp.float32
    )
    top = jnp.max(block_max, axis=0)
    factor = jnp.exp(block_max - top)
    top, total, numer = (
        top,
        jnp.sum(factor * totals, axis=0),
        jnp.sum(factor[..., None] * partial_out, axis=0),
    )
    attn = (
        jnp.transpose(numer / total[..., None], (1, 0, 2))
        .reshape(slab, local_heads * HD)
        .astype(jnp.bfloat16)
    )
    own_rows = x_tokens.shape[0]
    whole_terms = jnp.dot(attn, w_out, preferred_element_type=jnp.float32)
    summed = lax.psum(whole_terms.astype(jnp.bfloat16), "head").astype(jnp.float32)
    projected = lax.dynamic_slice_in_dim(summed, lax.axis_index("head") * own_rows, own_rows, 0)
    update = (projected * gate).astype(jnp.bfloat16)
    return (update, fresh_kv)


def _split_patch(mesh):
    patch = mesh.devices[:, 0]
    sizes = [len({d.coords[k] for d in patch}) for k in range(3)]
    sizes = [n for n in sizes if n > 1]
    if math.prod(sizes) != patch.shape[0] or len(sizes) < 2:
        return mesh, ("patch",)
    names = tuple(f"patch{k}" for k in range(len(sizes)))
    devices = mesh.devices.reshape(*sizes, mesh.devices.shape[1])
    return jax.sharding.Mesh(devices, names + ("head",)), names


PATCH = ("patch",)


def solution(mesh):
    global PATCH
    mesh, PATCH = _split_patch(mesh)
    placed = (
        P((*PATCH, "head"), None),
        P(),
        P(),
        P(),
        P(None, None, "head"),
        P("head", None),
        P("head"),
        P("head"),
        P(None, PATCH, "head"),
    )
    return jax.shard_map(
        per_device,
        mesh=mesh,
        in_specs=placed,
        out_specs=(P((*PATCH, "head"), None), P(None, PATCH, "head")),
        check_vma=False,
    )
```

```python
import math

import jax
import jax.numpy as jnp
from jax import lax
from jax.sharding import PartitionSpec as P

HD = 128


def modulate(x_tokens, shift, scale_mod):
    values_f = x_tokens.astype(jnp.float32)
    center = jnp.mean(values_f, axis=-1, keepdims=True)
    spread = jnp.mean((values_f - center) * (values_f - center), axis=-1, keepdims=True)
    return ((values_f - center) * lax.rsqrt(spread + 1e-06) * (1.0 + scale_mod) + shift).astype(
        jnp.bfloat16
    )


def per_device(x_tokens, shift, scale_mod, gate, w_qkv, w_out, gain_q, gain_k, stale_kv):
    normed = modulate(x_tokens, shift, scale_mod)
    width = w_qkv.shape[1]
    raw = jnp.einsum(
        "nd,cde->cne",
        lax.all_gather(normed, "head", axis=0, tiled=True),
        w_qkv,
        preferred_element_type=jnp.float32,
    )
    squares = jnp.sum(raw[:2] * raw[:2], axis=2)
    squares = lax.psum(squares, "head")
    inverse = lax.rsqrt(squares / width + 1e-06)
    queries = (raw[0] * inverse[0][:, None] * gain_q).astype(jnp.bfloat16)
    keys = (raw[1] * inverse[1][:, None] * gain_k).astype(jnp.bfloat16)
    values = raw[2].astype(jnp.bfloat16)
    fresh_kv = jnp.stack([keys, values])
    slab = queries.shape[0]
    local_heads = queries.shape[1] // HD
    own = lax.axis_index(PATCH)
    gathered = _gather_blocks(stale_kv)
    count = gathered.shape[1] // slab
    block_ids = jnp.arange(count, dtype=jnp.int32)
    is_own = (block_ids == own)[:, None]
    scale = math.sqrt(HD)
    heads_out = []
    for h in range(local_heads):
        cols = slice(h * HD, (h + 1) * HD)
        query = queries[:, cols]
        stale_k = gathered[0, :, cols].reshape(count, slab, HD)
        stale_v = gathered[1, :, cols].reshape(count, slab, HD)
        scores = jnp.einsum("qd,bkd->bqk", query, stale_k, preferred_element_type=jnp.float32) / scale
        block_max = jnp.max(scores, axis=-1)
        expo = jnp.exp(scores - block_max[..., None])
        totals = jnp.sum(expo, axis=-1)
        partial_out = jnp.einsum(
            "bqk,bkd->bqd", expo.astype(jnp.bfloat16), stale_v, preferred_element_type=jnp.float32
        )
        fresh_scores = jnp.einsum(
            "qd,kd->qk", query, keys[:, cols], preferred_element_type=jnp.float32
        ) / scale
        fresh_max = jnp.max(fresh_scores, axis=-1)
        fresh_expo = jnp.exp(fresh_scores - fresh_max[:, None])
        fresh_total = jnp.sum(fresh_expo, axis=-1)
        fresh_out = jnp.dot(
            fresh_expo.astype(jnp.bfloat16), values[:, cols], preferred_element_type=jnp.float32
        )
        top = jnp.maximum(jnp.max(jnp.where(is_own, -jnp.inf, block_max), axis=0), fresh_max)
        factor = jnp.where(is_own, 0.0, jnp.exp(block_max - top))
        fresh_factor = jnp.exp(fresh_max - top)
        total = jnp.sum(factor * totals, axis=0) + fresh_factor * fresh_total
        numer = jnp.sum(factor[..., None] * partial_out, axis=0) + fresh_factor[:, None] * fresh_out
        heads_out.append(numer / total[:, None])
    attn = jnp.concatenate(heads_out, axis=1).astype(jnp.bfloat16)
    own_rows = x_tokens.shape[0]
    groups = slab // own_rows
    whole_terms = jnp.dot(attn, w_out, preferred_element_type=jnp.float32).astype(jnp.bfloat16)
    pieces = lax.all_to_all(
        whole_terms.reshape(groups, own_rows, whole_terms.shape[1]), "head", 0, 0, tiled=True
    )
    projected = jnp.sum(pieces.astype(jnp.float32), axis=0)
    update = (projected * gate).astype(jnp.bfloat16)
    return (update, fresh_kv)


def _gather_blocks(stale_kv):
    inner = PATCH[-1]
    if len(PATCH) == 1:
        return lax.all_gather(stale_kv, inner, axis=1, tiled=True)
    n = lax.psum(1, inner)
    spread = jnp.broadcast_to(stale_kv[:, None], (2, n) + stale_kv.shape[1:])
    spread = spread.reshape(2, n * stale_kv.shape[1], stale_kv.shape[2])
    near = lax.all_to_all(spread, inner, 1, 1, tiled=True)
    return lax.all_gather(near, PATCH[:-1], axis=1, tiled=True)


def _split_patch(mesh):
    patch = mesh.devices[:, 0]
    sizes = [len({d.coords[k] for d in patch}) for k in range(3)]
    sizes = [n for n in sizes if n > 1]
    if math.prod(sizes) != patch.shape[0] or len(sizes) < 2:
        return mesh, ("patch",)
    names = tuple(f"patch{k}" for k in range(len(sizes)))
    devices = mesh.devices.reshape(*sizes, mesh.devices.shape[1])
    return jax.sharding.Mesh(devices, names + ("head",)), names


PATCH = ("patch",)


def solution(mesh):
    global PATCH
    mesh, PATCH = _split_patch(mesh)
    placed = (
        P((*PATCH, "head"), None),
        P(),
        P(),
        P(),
        P(None, None, "head"),
        P("head", None),
        P("head"),
        P("head"),
        P(None, PATCH, "head"),
    )
    return jax.shard_map(
        per_device,
        mesh=mesh,
        in_specs=placed,
        out_specs=(P((*PATCH, "head"), None), P(None, PATCH, "head")),
        check_vma=False,
    )
```

```python
import math

import jax
import jax.numpy as jnp
from jax import lax
from jax.sharding import PartitionSpec as P

HD = 128


def modulate(x_tokens, shift, scale_mod):
    values_f = x_tokens.astype(jnp.float32)
    center = jnp.mean(values_f, axis=-1, keepdims=True)
    spread = jnp.mean((values_f - center) * (values_f - center), axis=-1, keepdims=True)
    return ((values_f - center) * lax.rsqrt(spread + 1e-06) * (1.0 + scale_mod) + shift).astype(
        jnp.bfloat16
    )


def per_device(x_tokens, shift, scale_mod, gate, w_qkv, w_out, gain_q, gain_k, stale_kv):
    normed = modulate(x_tokens, shift, scale_mod)
    width = w_qkv.shape[1]
    raw = jnp.einsum(
        "nd,cde->cne",
        lax.all_gather(normed, "head", axis=0, tiled=True),
        w_qkv,
        preferred_element_type=jnp.float32,
    )
    squares = jnp.sum(raw[:2] * raw[:2], axis=2)
    squares = lax.psum(squares, "head")
    inverse = lax.rsqrt(squares / width + 1e-06)
    queries = (raw[0] * inverse[0][:, None] * gain_q).astype(jnp.bfloat16)
    keys = (raw[1] * inverse[1][:, None] * gain_k).astype(jnp.bfloat16)
    values = raw[2].astype(jnp.bfloat16)
    fresh_kv = jnp.stack([keys, values])
    slab = queries.shape[0]
    local_heads = queries.shape[1] // HD
    own = lax.axis_index(PATCH)
    stale_keys = _gather_blocks(stale_kv[0])
    stale_values = _gather_blocks(stale_kv[1])
    count = stale_keys.shape[0] // slab
    block_ids = jnp.arange(count, dtype=jnp.int32)
    is_own = (block_ids == own)[:, None]
    scale = math.sqrt(HD)
    heads_out = []
    for h in range(local_heads):
        cols = slice(h * HD, (h + 1) * HD)
        query = queries[:, cols]
        stale_k = stale_keys[:, cols].reshape(count, slab, HD)
        stale_v = stale_values[:, cols].reshape(count, slab, HD)
        scores = jnp.einsum("qd,bkd->bqk", query, stale_k, preferred_element_type=jnp.float32) / scale
        block_max = jnp.max(scores, axis=-1)
        expo = jnp.exp(scores - block_max[..., None])
        totals = jnp.sum(expo, axis=-1)
        partial_out = jnp.einsum(
            "bqk,bkd->bqd", expo.astype(jnp.bfloat16), stale_v, preferred_element_type=jnp.float32
        )
        fresh_scores = jnp.einsum(
            "qd,kd->qk", query, keys[:, cols], preferred_element_type=jnp.float32
        ) / scale
        fresh_max = jnp.max(fresh_scores, axis=-1)
        fresh_expo = jnp.exp(fresh_scores - fresh_max[:, None])
        fresh_total = jnp.sum(fresh_expo, axis=-1)
        fresh_out = jnp.dot(
            fresh_expo.astype(jnp.bfloat16), values[:, cols], preferred_element_type=jnp.float32
        )
        top = jnp.maximum(jnp.max(jnp.where(is_own, -jnp.inf, block_max), axis=0), fresh_max)
        factor = jnp.where(is_own, 0.0, jnp.exp(block_max - top))
        fresh_factor = jnp.exp(fresh_max - top)
        total = jnp.sum(factor * totals, axis=0) + fresh_factor * fresh_total
        numer = jnp.sum(factor[..., None] * partial_out, axis=0) + fresh_factor[:, None] * fresh_out
        heads_out.append(numer / total[:, None])
    attn = jnp.concatenate(heads_out, axis=1).astype(jnp.bfloat16)
    own_rows = x_tokens.shape[0]
    groups = slab // own_rows
    whole_terms = jnp.dot(attn, w_out, preferred_element_type=jnp.float32).astype(jnp.bfloat16)
    pieces = lax.all_to_all(
        whole_terms.reshape(groups, own_rows, whole_terms.shape[1]), "head", 0, 0, tiled=True
    )
    projected = jnp.sum(pieces.astype(jnp.float32), axis=0)
    update = (projected * gate).astype(jnp.bfloat16)
    return (update, fresh_kv)


def _gather_blocks(stale):
    inner = PATCH[-1]
    if len(PATCH) == 1:
        return lax.all_gather(stale, inner, axis=0, tiled=True)
    n = lax.psum(1, inner)
    spread = jnp.broadcast_to(stale[None], (n,) + stale.shape).reshape(n * stale.shape[0], stale.shape[1])
    near = lax.all_to_all(spread, inner, 0, 0, tiled=True)
    return lax.all_gather(near, PATCH[:-1], axis=0, tiled=True)


def _split_patch(mesh):
    patch = mesh.devices[:, 0]
    sizes = [len({d.coords[k] for d in patch}) for k in range(3)]
    sizes = [n for n in sizes if n > 1]
    if math.prod(sizes) != patch.shape[0] or len(sizes) < 2:
        return mesh, ("patch",)
    names = tuple(f"patch{k}" for k in range(len(sizes)))
    devices = mesh.devices.reshape(*sizes, mesh.devices.shape[1])
    return jax.sharding.Mesh(devices, names + ("head",)), names


PATCH = ("patch",)


def solution(mesh):
    global PATCH
    mesh, PATCH = _split_patch(mesh)
    placed = (
        P((*PATCH, "head"), None),
        P(),
        P(),
        P(),
        P(None, None, "head"),
        P("head", None),
        P("head"),
        P("head"),
        P(None, PATCH, "head"),
    )
    return jax.shard_map(
        per_device,
        mesh=mesh,
        in_specs=placed,
        out_specs=(P((*PATCH, "head"), None), P(None, PATCH, "head")),
        check_vma=False,
    )
```

```python
import math

import jax
import jax.numpy as jnp
from jax import lax
from jax.experimental import pallas as pl
from jax.experimental.pallas import tpu as pltpu
from jax.sharding import PartitionSpec as P

HD = 128


def modulate(x_tokens, shift, scale_mod):
    values_f = x_tokens.astype(jnp.float32)
    center = jnp.mean(values_f, axis=-1, keepdims=True)
    spread = jnp.mean((values_f - center) * (values_f - center), axis=-1, keepdims=True)
    return ((values_f - center) * lax.rsqrt(spread + 1e-06) * (1.0 + scale_mod) + shift).astype(
        jnp.bfloat16
    )


def per_device(x_tokens, shift, scale_mod, gate, w_qkv, w_out, gain_q, gain_k, stale_kv):
    normed = modulate(x_tokens, shift, scale_mod)
    width = w_qkv.shape[1]
    raw = jnp.einsum(
        "nd,cde->cne",
        lax.all_gather(normed, "head", axis=0, tiled=True),
        w_qkv,
        preferred_element_type=jnp.float32,
    )
    squares = jnp.sum(raw[:2] * raw[:2], axis=2)
    squares = lax.psum(squares, "head")
    inverse = lax.rsqrt(squares / width + 1e-06)
    queries = (raw[0] * inverse[0][:, None] * gain_q).astype(jnp.bfloat16)
    keys = (raw[1] * inverse[1][:, None] * gain_k).astype(jnp.bfloat16)
    values = raw[2].astype(jnp.bfloat16)
    fresh_kv = jnp.stack([keys, values])
    own = lax.axis_index(PATCH).astype(jnp.int32).reshape(1)
    gathered = _gather_blocks(stale_kv)
    attn = _attention(own, queries, keys, values, gathered)
    own_rows = x_tokens.shape[0]
    groups = queries.shape[0] // own_rows
    whole_terms = jnp.dot(attn, w_out, preferred_element_type=jnp.float32).astype(jnp.bfloat16)
    pieces = lax.all_to_all(
        whole_terms.reshape(groups, own_rows, whole_terms.shape[1]), "head", 0, 0, tiled=True
    )
    projected = jnp.sum(pieces.astype(jnp.float32), axis=0)
    update = (projected * gate).astype(jnp.bfloat16)
    return (update, fresh_kv)


def _attention_kernel(own_ref, q_ref, k_ref, v_ref, kv_ref, out_ref):
    slab = q_ref.shape[0]
    count = kv_ref.shape[1] // slab
    scale = math.sqrt(HD)
    is_own = lax.broadcasted_iota(jnp.int32, (count, 1), 0) == own_ref[0]
    contract_minor = (((1,), (1,)), ((), ()))
    contract_major = (((0,), (0,)), ((), ()))
    for h in range(q_ref.shape[1] // HD):
        cols = pl.ds(h * HD, HD)
        query = q_ref[:, cols]
        scores = lax.dot_general(
            kv_ref[0, :, cols], query, contract_minor, preferred_element_type=jnp.float32
        ) / scale
        scores = scores.reshape(count, slab, slab)
        block_max = jnp.max(scores, axis=1)
        expo = jnp.exp(scores - block_max[:, None, :])
        totals = jnp.sum(expo, axis=1)
        weights = expo.astype(jnp.bfloat16).astype(jnp.float32)
        fresh_scores = lax.dot_general(
            k_ref[:, cols], query, contract_minor, preferred_element_type=jnp.float32
        ) / scale
        fresh_max = jnp.max(fresh_scores, axis=0, keepdims=True)
        fresh_expo = jnp.exp(fresh_scores - fresh_max)
        fresh_total = jnp.sum(fresh_expo, axis=0, keepdims=True)
        fresh_weights = fresh_expo.astype(jnp.bfloat16).astype(jnp.float32)
        top = jnp.maximum(
            jnp.max(jnp.where(is_own, -jnp.inf, block_max), axis=0, keepdims=True), fresh_max
        )
        factor = jnp.where(is_own, 0.0, jnp.exp(block_max - top))
        fresh_factor = jnp.exp(fresh_max - top)
        total = jnp.sum(factor * totals, axis=0, keepdims=True) + fresh_factor * fresh_total
        mixed = (factor[:, None, :] * weights).reshape(count * slab, slab)
        numer = lax.dot_general(
            mixed,
            kv_ref[1, :, cols].astype(jnp.float32),
            contract_major,
            preferred_element_type=jnp.float32,
            precision=lax.Precision.HIGHEST,
        )
        numer = numer + lax.dot_general(
            fresh_factor * fresh_weights,
            v_ref[:, cols].astype(jnp.float32),
            contract_major,
            preferred_element_type=jnp.float32,
            precision=lax.Precision.HIGHEST,
        )
        out_ref[:, cols] = (numer / total.reshape(slab, 1)).astype(out_ref.dtype)


def _attention(own, queries, keys, values, gathered):
    vmem = pl.BlockSpec(memory_space=pltpu.VMEM)
    return pl.pallas_call(
        _attention_kernel,
        out_shape=jax.ShapeDtypeStruct(queries.shape, jnp.bfloat16),
        in_specs=[pl.BlockSpec(memory_space=pltpu.SMEM), vmem, vmem, vmem, vmem],
        out_specs=vmem,
        compiler_params=pltpu.CompilerParams(vmem_limit_bytes=48 * 1024 * 1024),
    )(own, queries, keys, values, gathered)


def _gather_blocks(stale_kv):
    inner = PATCH[-1]
    if len(PATCH) == 1:
        return lax.all_gather(stale_kv, inner, axis=1, tiled=True)
    n = lax.psum(1, inner)
    spread = jnp.broadcast_to(stale_kv[:, None], (2, n) + stale_kv.shape[1:])
    spread = spread.reshape(2, n * stale_kv.shape[1], stale_kv.shape[2])
    near = lax.all_to_all(spread, inner, 1, 1, tiled=True)
    return lax.all_gather(near, PATCH[:-1], axis=1, tiled=True)


def _split_patch(mesh):
    patch = mesh.devices[:, 0]
    sizes = [len({d.coords[k] for d in patch}) for k in range(3)]
    sizes = [n for n in sizes if n > 1]
    if math.prod(sizes) != patch.shape[0] or len(sizes) < 2:
        return mesh, ("patch",)
    names = tuple(f"patch{k}" for k in range(len(sizes)))
    devices = mesh.devices.reshape(*sizes, mesh.devices.shape[1])
    return jax.sharding.Mesh(devices, names + ("head",)), names


PATCH = ("patch",)


def solution(mesh):
    global PATCH
    mesh, PATCH = _split_patch(mesh)
    placed = (
        P((*PATCH, "head"), None),
        P(),
        P(),
        P(),
        P(None, None, "head"),
        P("head", None),
        P("head"),
        P("head"),
        P(None, PATCH, "head"),
    )
    return jax.shard_map(
        per_device,
        mesh=mesh,
        in_specs=placed,
        out_specs=(P((*PATCH, "head"), None), P(None, PATCH, "head")),
        check_vma=False,
    )
```

```python
import math

import jax
import jax.numpy as jnp
from jax import lax
from jax.experimental import pallas as pl
from jax.experimental.pallas import tpu as pltpu
from jax.sharding import PartitionSpec as P

HD = 128


def modulate(x_tokens, shift, scale_mod):
    values_f = x_tokens.astype(jnp.float32)
    center = jnp.mean(values_f, axis=-1, keepdims=True)
    spread = jnp.mean((values_f - center) * (values_f - center), axis=-1, keepdims=True)
    return ((values_f - center) * lax.rsqrt(spread + 1e-06) * (1.0 + scale_mod) + shift).astype(
        jnp.bfloat16
    )


def per_device(x_tokens, shift, scale_mod, gate, w_qkv, w_out, gain_q, gain_k, stale_kv):
    normed = modulate(x_tokens, shift, scale_mod)
    width = w_qkv.shape[1]
    raw = jnp.einsum(
        "nd,cde->cne",
        lax.all_gather(normed, "head", axis=0, tiled=True),
        w_qkv,
        preferred_element_type=jnp.float32,
    )
    squares = jnp.sum(raw[:2] * raw[:2], axis=2)
    squares = lax.psum(squares, "head")
    inverse = lax.rsqrt(squares / width + 1e-06)
    queries = (raw[0] * inverse[0][:, None] * gain_q).astype(jnp.bfloat16)
    keys = (raw[1] * inverse[1][:, None] * gain_k).astype(jnp.bfloat16)
    values = raw[2].astype(jnp.bfloat16)
    fresh_kv = jnp.stack([keys, values])
    attn = _exchange_attention(stale_kv, queries, keys, values)
    own_rows = x_tokens.shape[0]
    groups = queries.shape[0] // own_rows
    whole_terms = jnp.dot(attn, w_out, preferred_element_type=jnp.float32).astype(jnp.bfloat16)
    pieces = lax.all_to_all(
        whole_terms.reshape(groups, own_rows, whole_terms.shape[1]), "head", 0, 0, tiled=True
    )
    projected = jnp.sum(pieces.astype(jnp.float32), axis=0)
    update = (projected * gate).astype(jnp.bfloat16)
    return (update, fresh_kv)


def _partial_kernel(mask_ref, q_ref, k_ref, v_ref, kv_ref, out_ref):
    queries_n = q_ref.shape[0]
    slab = k_ref.shape[0]
    count = kv_ref.shape[1] // slab
    heads = q_ref.shape[1] // HD
    scale = math.sqrt(HD)
    is_own = mask_ref[...] > 0
    fresh_col = jnp.max(mask_ref[...], axis=0, keepdims=True) > 0
    contract_minor = (((1,), (1,)), ((), ()))
    contract_major = (((0,), (0,)), ((), ()))
    lane = lax.broadcasted_iota(jnp.int32, (queries_n, HD), 1)
    stats = jnp.zeros((queries_n, HD), jnp.float32)
    for h in range(heads):
        cols = pl.ds(h * HD, HD)
        query = q_ref[:, cols]
        scores = lax.dot_general(
            kv_ref[0, :, cols].astype(jnp.bfloat16), query, contract_minor,
            preferred_element_type=jnp.float32,
        ) / scale
        scores = scores.reshape(count, slab, queries_n)
        block_max = jnp.max(scores, axis=1)
        expo = jnp.exp(scores - block_max[:, None, :])
        totals = jnp.sum(expo, axis=1)
        weights = expo.astype(jnp.bfloat16).astype(jnp.float32)
        fresh_scores = lax.dot_general(
            k_ref[:, cols], query, contract_minor, preferred_element_type=jnp.float32
        ) / scale
        fresh_max = jnp.max(fresh_scores, axis=0, keepdims=True)
        fresh_expo = jnp.exp(fresh_scores - fresh_max)
        fresh_total = jnp.sum(fresh_expo, axis=0, keepdims=True)
        fresh_weights = fresh_expo.astype(jnp.bfloat16).astype(jnp.float32)
        top = jnp.max(jnp.where(is_own, -jnp.inf, block_max), axis=0, keepdims=True)
        top = jnp.maximum(top, jnp.where(fresh_col, fresh_max, -jnp.inf))
        factor = jnp.where(is_own, 0.0, jnp.exp(block_max - top))
        fresh_factor = jnp.where(fresh_col, jnp.exp(fresh_max - top), 0.0)
        total = jnp.sum(factor * totals, axis=0, keepdims=True) + fresh_factor * fresh_total
        mixed = (factor[:, None, :] * weights).reshape(count * slab, queries_n)
        numer = lax.dot_general(
            mixed,
            kv_ref[1, :, cols],
            contract_major,
            preferred_element_type=jnp.float32,
            precision=lax.Precision.HIGHEST,
        )
        numer = numer + lax.dot_general(
            fresh_factor * fresh_weights,
            v_ref[:, cols].astype(jnp.float32),
            contract_major,
            preferred_element_type=jnp.float32,
            precision=lax.Precision.HIGHEST,
        )
        out_ref[:, cols] = numer
        stats = jnp.where(lane == h, top.reshape(queries_n, 1), stats)
        stats = jnp.where(lane == 4 + h, total.reshape(queries_n, 1), stats)
    out_ref[:, pl.ds(heads * HD, HD)] = stats


def _partial_attention(mask, group_queries, keys, values, near_kv):
    vmem = pl.BlockSpec(memory_space=pltpu.VMEM)
    rows, width = group_queries.shape
    return pl.pallas_call(
        _partial_kernel,
        out_shape=jax.ShapeDtypeStruct((rows, width + HD), jnp.float32),
        in_specs=[vmem] * 5,
        out_specs=vmem,
        compiler_params=pltpu.CompilerParams(vmem_limit_bytes=48 * 1024 * 1024),
    )(mask, group_queries, keys, values, near_kv)


def _exchange_attention(stale_kv, queries, keys, values):
    slab, width = queries.shape
    heads = width // HD
    outer, inner = PATCH[:-1], PATCH[-1]
    near_kv = lax.all_gather(stale_kv.astype(jnp.float32), outer, axis=1, tiled=True)
    count = near_kv.shape[1] // slab
    n = lax.psum(1, inner)
    spread = jnp.broadcast_to(queries[None], (n, slab, width)).reshape(n * slab, width)
    group_queries = lax.all_to_all(spread, inner, 0, 0, tiled=True)
    block_ids = jnp.arange(count, dtype=jnp.int32)[:, None]
    slab_ids = (jnp.arange(n * slab, dtype=jnp.int32) // slab)[None, :]
    mask = ((block_ids == lax.axis_index(outer)) & (slab_ids == lax.axis_index(inner))).astype(jnp.int32)
    partial = _partial_attention(mask, group_queries, keys, values, near_kv)
    parts = lax.all_to_all(partial.reshape(n, slab, width + HD), inner, 0, 0, tiled=True)
    tops = parts[:, :, width : width + heads]
    totals = parts[:, :, width + 4 : width + 4 + heads]
    top = jnp.max(tops, axis=0)
    factor = jnp.exp(tops - top)
    total = jnp.sum(factor * totals, axis=0)
    numer = jnp.sum(factor[..., None] * parts[:, :, :width].reshape(n, slab, heads, HD), axis=0)
    return (numer / total[..., None]).reshape(slab, width).astype(jnp.bfloat16)


def _split_patch(mesh):
    patch = mesh.devices[:, 0]
    sizes = [len({d.coords[k] for d in patch}) for k in range(3)]
    sizes = [n for n in sizes if n > 1]
    if math.prod(sizes) != patch.shape[0] or len(sizes) < 2:
        return mesh, ("patch",)
    names = tuple(f"patch{k}" for k in range(len(sizes)))
    devices = mesh.devices.reshape(*sizes, mesh.devices.shape[1])
    return jax.sharding.Mesh(devices, names + ("head",)), names


PATCH = ("patch",)


def solution(mesh):
    global PATCH
    mesh, PATCH = _split_patch(mesh)
    placed = (
        P((*PATCH, "head"), None),
        P(),
        P(),
        P(),
        P(None, None, "head"),
        P("head", None),
        P("head"),
        P("head"),
        P(None, PATCH, "head"),
    )
    return jax.shard_map(
        per_device,
        mesh=mesh,
        in_specs=placed,
        out_specs=(P((*PATCH, "head"), None), P(None, PATCH, "head")),
        check_vma=False,
    )
```

```python
import math

import jax
import jax.numpy as jnp
from jax import lax
from jax.experimental import pallas as pl
from jax.experimental.pallas import tpu as pltpu
from jax.sharding import PartitionSpec as P

HD = 128


def modulate(x_tokens, shift, scale_mod):
    values_f = x_tokens.astype(jnp.float32)
    center = jnp.mean(values_f, axis=-1, keepdims=True)
    spread = jnp.mean((values_f - center) * (values_f - center), axis=-1, keepdims=True)
    return ((values_f - center) * lax.rsqrt(spread + 1e-06) * (1.0 + scale_mod) + shift).astype(
        jnp.bfloat16
    )


def per_device(x_tokens, shift, scale_mod, gate, w_qkv, w_out, gain_q, gain_k, stale_kv):
    normed = modulate(x_tokens, shift, scale_mod)
    width = w_qkv.shape[1]
    raw = jnp.einsum(
        "nd,cde->cne",
        lax.all_gather(normed, "head", axis=0, tiled=True),
        w_qkv,
        preferred_element_type=jnp.float32,
    )
    squares = jnp.sum(raw[:2] * raw[:2], axis=2)
    squares = jnp.sum(lax.all_gather(squares, "head"), axis=0)
    inverse = lax.rsqrt(squares / width + 1e-06)
    queries = (raw[0] * inverse[0][:, None] * gain_q).astype(jnp.bfloat16)
    keys = (raw[1] * inverse[1][:, None] * gain_k).astype(jnp.bfloat16)
    values = raw[2].astype(jnp.bfloat16)
    fresh_kv = jnp.stack([keys, values])
    attn = _exchange_attention(stale_kv, queries, keys, values)
    own_rows = x_tokens.shape[0]
    groups = queries.shape[0] // own_rows
    whole_terms = jnp.dot(attn, w_out, preferred_element_type=jnp.float32).astype(jnp.bfloat16)
    pieces = lax.all_to_all(
        whole_terms.reshape(groups, own_rows, whole_terms.shape[1]), "head", 0, 0, tiled=True
    )
    projected = jnp.sum(pieces.astype(jnp.float32), axis=0)
    update = (projected * gate).astype(jnp.bfloat16)
    return (update, fresh_kv)


def _partial_kernel(mask_ref, q_ref, k_ref, v_ref, kv_ref, out_ref, weight_ref):
    queries_n = q_ref.shape[0]
    slab = k_ref.shape[0]
    count = kv_ref.shape[1] // slab
    heads = q_ref.shape[1] // HD
    scale = math.sqrt(HD)
    is_own = mask_ref[...] > 0
    fresh_col = jnp.max(mask_ref[...], axis=0, keepdims=True) > 0
    contract_minor = (((1,), (1,)), ((), ()))
    contract_major = (((0,), (0,)), ((), ()))
    weight_ref[...] = jnp.zeros(weight_ref.shape, jnp.float32)
    for h in range(heads):
        cols = pl.ds(h * HD, HD)
        query = q_ref[:, cols]
        scores = lax.dot_general(
            kv_ref[0, :, cols].astype(jnp.bfloat16), query, contract_minor,
            preferred_element_type=jnp.float32,
        ) / scale
        scores = scores.reshape(count, slab, queries_n)
        block_max = jnp.max(scores, axis=1)
        expo = jnp.exp(scores - block_max[:, None, :])
        totals = jnp.sum(expo, axis=1)
        weights = expo.astype(jnp.bfloat16).astype(jnp.float32)
        fresh_scores = lax.dot_general(
            k_ref[:, cols], query, contract_minor, preferred_element_type=jnp.float32
        ) / scale
        fresh_max = jnp.max(fresh_scores, axis=0, keepdims=True)
        fresh_expo = jnp.exp(fresh_scores - fresh_max)
        fresh_total = jnp.sum(fresh_expo, axis=0, keepdims=True)
        fresh_weights = fresh_expo.astype(jnp.bfloat16).astype(jnp.float32)
        top = jnp.max(jnp.where(is_own, -jnp.inf, block_max), axis=0, keepdims=True)
        top = jnp.maximum(top, jnp.where(fresh_col, fresh_max, -jnp.inf))
        factor = jnp.where(is_own, 0.0, jnp.exp(block_max - top))
        fresh_factor = jnp.where(fresh_col, jnp.exp(fresh_max - top), 0.0)
        total = jnp.sum(factor * totals, axis=0, keepdims=True) + fresh_factor * fresh_total
        mixed = (factor[:, None, :] * weights).reshape(count * slab, queries_n)
        numer = lax.dot_general(
            mixed,
            kv_ref[1, :, cols],
            contract_major,
            preferred_element_type=jnp.float32,
            precision=lax.Precision.HIGHEST,
        )
        numer = numer + lax.dot_general(
            fresh_factor * fresh_weights,
            v_ref[:, cols].astype(jnp.float32),
            contract_major,
            preferred_element_type=jnp.float32,
            precision=lax.Precision.HIGHEST,
        )
        out_ref[:, cols] = (numer / total.reshape(queries_n, 1)).astype(out_ref.dtype)
        weight_ref[pl.ds(h, 1), :] = top + jnp.log(total)


def _partial_attention(mask, group_queries, keys, values, near_kv):
    vmem = pl.BlockSpec(memory_space=pltpu.VMEM)
    rows, width = group_queries.shape
    return pl.pallas_call(
        _partial_kernel,
        out_shape=(
            jax.ShapeDtypeStruct((rows, width), jnp.bfloat16),
            jax.ShapeDtypeStruct((8, rows), jnp.float32),
        ),
        in_specs=[vmem] * 5,
        out_specs=(vmem, vmem),
        compiler_params=pltpu.CompilerParams(vmem_limit_bytes=48 * 1024 * 1024),
    )(mask, group_queries, keys, values, near_kv)


def _exchange_attention(stale_kv, queries, keys, values):
    slab, width = queries.shape
    heads = width // HD
    outer, inner = PATCH[:-1], PATCH[-1]
    near_kv = lax.all_gather(stale_kv.astype(jnp.float32), outer, axis=1, tiled=True)
    count = near_kv.shape[1] // slab
    n = lax.psum(1, inner)
    spread = jnp.broadcast_to(queries[None], (n, slab, width)).reshape(n * slab, width)
    group_queries = lax.all_to_all(spread, inner, 0, 0, tiled=True)
    block_ids = jnp.arange(count, dtype=jnp.int32)[:, None]
    slab_ids = (jnp.arange(n * slab, dtype=jnp.int32) // slab)[None, :]
    mask = ((block_ids == lax.axis_index(outer)) & (slab_ids == lax.axis_index(inner))).astype(jnp.int32)
    partial, log_weight = _partial_attention(mask, group_queries, keys, values, near_kv)
    parts = lax.all_to_all(partial.reshape(n, slab, width), inner, 0, 0, tiled=True)
    log_weight = log_weight[:heads].reshape(heads, n, slab).transpose(1, 0, 2)
    log_weight = lax.all_to_all(log_weight, inner, 0, 0, tiled=True)
    top = jnp.max(log_weight, axis=0)
    factor = jnp.exp(log_weight - top)
    total = jnp.sum(factor, axis=0)
    numer = jnp.sum(
        factor.transpose(0, 2, 1)[..., None] * parts.reshape(n, slab, heads, HD).astype(jnp.float32),
        axis=0,
    )
    total = total.T
    return (numer / total[..., None]).reshape(slab, width).astype(jnp.bfloat16)


def _split_patch(mesh):
    patch = mesh.devices[:, 0]
    sizes = [len({d.coords[k] for d in patch}) for k in range(3)]
    sizes = [n for n in sizes if n > 1]
    if math.prod(sizes) != patch.shape[0] or len(sizes) < 2:
        return mesh, ("patch",)
    names = tuple(f"patch{k}" for k in range(len(sizes)))
    devices = mesh.devices.reshape(*sizes, mesh.devices.shape[1])
    return jax.sharding.Mesh(devices, names + ("head",)), names


PATCH = ("patch",)


def solution(mesh):
    global PATCH
    mesh, PATCH = _split_patch(mesh)
    placed = (
        P((*PATCH, "head"), None),
        P(),
        P(),
        P(),
        P(None, None, "head"),
        P("head", None),
        P("head"),
        P("head"),
        P(None, PATCH, "head"),
    )
    return jax.shard_map(
        per_device,
        mesh=mesh,
        in_specs=placed,
        out_specs=(P((*PATCH, "head"), None), P(None, PATCH, "head")),
        check_vma=False,
    )
```

```python
import math

import jax
import jax.numpy as jnp
from jax import lax
from jax.experimental import pallas as pl
from jax.experimental.pallas import tpu as pltpu
from jax.sharding import PartitionSpec as P

HD = 128


def modulate(x_tokens, shift, scale_mod):
    values_f = x_tokens.astype(jnp.float32)
    center = jnp.mean(values_f, axis=-1, keepdims=True)
    spread = jnp.mean((values_f - center) * (values_f - center), axis=-1, keepdims=True)
    return ((values_f - center) * lax.rsqrt(spread + 1e-06) * (1.0 + scale_mod) + shift).astype(
        jnp.bfloat16
    )


def per_device(x_tokens, shift, scale_mod, gate, w_qkv, w_out, gain_q, gain_k, stale_kv):
    normed = modulate(x_tokens, shift, scale_mod)
    width = w_qkv.shape[1]
    raw = jnp.einsum(
        "nd,cde->cne",
        lax.all_gather(normed, "head", axis=0, tiled=True),
        w_qkv,
        preferred_element_type=jnp.float32,
    )
    squares = jnp.sum(raw[:2] * raw[:2], axis=2)
    squares = jnp.sum(lax.all_gather(squares, "head"), axis=0)
    inverse = lax.rsqrt(squares / width + 1e-06)
    queries = (raw[0] * inverse[0][:, None] * gain_q).astype(jnp.bfloat16)
    keys = (raw[1] * inverse[1][:, None] * gain_k).astype(jnp.bfloat16)
    values = raw[2].astype(jnp.bfloat16)
    fresh_kv = jnp.stack([keys, values])
    parts, log_weight = _exchange_attention(stale_kv, queries, keys, values)
    own_rows = x_tokens.shape[0]
    groups = queries.shape[0] // own_rows
    whole_terms = _combine_project(parts, log_weight, w_out)
    pieces = lax.all_to_all(
        whole_terms.reshape(groups, own_rows, whole_terms.shape[1]), "head", 0, 0, tiled=True
    )
    projected = jnp.sum(pieces.astype(jnp.float32), axis=0)
    update = (projected * gate).astype(jnp.bfloat16)
    return (update, fresh_kv)


def _partial_kernel(mask_ref, q_ref, k_ref, v_ref, kv_ref, out_ref, weight_ref):
    queries_n = q_ref.shape[0]
    slab = k_ref.shape[0]
    count = kv_ref.shape[1] // slab
    heads = q_ref.shape[1] // HD
    scale = math.sqrt(HD)
    is_own = mask_ref[...] > 0
    fresh_col = jnp.max(mask_ref[...], axis=0, keepdims=True) > 0
    contract_minor = (((1,), (1,)), ((), ()))
    contract_major = (((0,), (0,)), ((), ()))
    weight_ref[...] = jnp.zeros(weight_ref.shape, jnp.float32)
    for h in range(heads):
        cols = pl.ds(h * HD, HD)
        query = q_ref[:, cols]
        scores = lax.dot_general(
            kv_ref[0, :, cols].astype(jnp.bfloat16), query, contract_minor,
            preferred_element_type=jnp.float32,
        ) / scale
        scores = scores.reshape(count, slab, queries_n)
        block_max = jnp.max(scores, axis=1)
        expo = jnp.exp(scores - block_max[:, None, :])
        totals = jnp.sum(expo, axis=1)
        weights = expo.astype(jnp.bfloat16).astype(jnp.float32)
        fresh_scores = lax.dot_general(
            k_ref[:, cols], query, contract_minor, preferred_element_type=jnp.float32
        ) / scale
        fresh_max = jnp.max(fresh_scores, axis=0, keepdims=True)
        fresh_expo = jnp.exp(fresh_scores - fresh_max)
        fresh_total = jnp.sum(fresh_expo, axis=0, keepdims=True)
        fresh_weights = fresh_expo.astype(jnp.bfloat16).astype(jnp.float32)
        top = jnp.max(jnp.where(is_own, -jnp.inf, block_max), axis=0, keepdims=True)
        top = jnp.maximum(top, jnp.where(fresh_col, fresh_max, -jnp.inf))
        factor = jnp.where(is_own, 0.0, jnp.exp(block_max - top))
        fresh_factor = jnp.where(fresh_col, jnp.exp(fresh_max - top), 0.0)
        total = jnp.sum(factor * totals, axis=0, keepdims=True) + fresh_factor * fresh_total
        mixed = (factor[:, None, :] * weights).reshape(count * slab, queries_n)
        numer = lax.dot_general(
            mixed,
            kv_ref[1, :, cols],
            contract_major,
            preferred_element_type=jnp.float32,
            precision=lax.Precision.HIGHEST,
        )
        numer = numer + lax.dot_general(
            fresh_factor * fresh_weights,
            v_ref[:, cols].astype(jnp.float32),
            contract_major,
            preferred_element_type=jnp.float32,
            precision=lax.Precision.HIGHEST,
        )
        out_ref[:, cols] = (numer / total.reshape(queries_n, 1)).astype(out_ref.dtype)
        weight_ref[pl.ds(h, 1), :] = top + jnp.log(total)


def _partial_attention(mask, group_queries, keys, values, near_kv):
    vmem = pl.BlockSpec(memory_space=pltpu.VMEM)
    rows, width = group_queries.shape
    return pl.pallas_call(
        _partial_kernel,
        out_shape=(
            jax.ShapeDtypeStruct((rows, width), jnp.bfloat16),
            jax.ShapeDtypeStruct((8, rows), jnp.float32),
        ),
        in_specs=[vmem] * 5,
        out_specs=(vmem, vmem),
        compiler_params=pltpu.CompilerParams(vmem_limit_bytes=48 * 1024 * 1024),
    )(mask, group_queries, keys, values, near_kv)


def _exchange_attention(stale_kv, queries, keys, values):
    slab, width = queries.shape
    heads = width // HD
    outer, inner = PATCH[:-1], PATCH[-1]
    near_kv = lax.all_gather(stale_kv.astype(jnp.float32), outer, axis=1, tiled=True)
    count = near_kv.shape[1] // slab
    n = lax.psum(1, inner)
    spread = jnp.broadcast_to(queries[None], (n, slab, width)).reshape(n * slab, width)
    group_queries = lax.all_to_all(spread, inner, 0, 0, tiled=True)
    block_ids = jnp.arange(count, dtype=jnp.int32)[:, None]
    slab_ids = (jnp.arange(n * slab, dtype=jnp.int32) // slab)[None, :]
    mask = ((block_ids == lax.axis_index(outer)) & (slab_ids == lax.axis_index(inner))).astype(jnp.int32)
    partial, log_weight = _partial_attention(mask, group_queries, keys, values, near_kv)
    parts = lax.all_to_all(partial.reshape(n, slab, width), inner, 0, 0, tiled=True)
    log_weight = log_weight[:heads].reshape(heads, n, slab).transpose(1, 0, 2)
    log_weight = lax.all_to_all(log_weight, inner, 0, 0, tiled=True)
    return parts, log_weight


def _combine_kernel(parts_ref, weight_ref, w_ref, out_ref):
    n, slab, width = parts_ref.shape
    columns = []
    for h in range(width // HD):
        log_weight = weight_ref[:, h, :]
        top = jnp.max(log_weight, axis=0, keepdims=True)
        factor = jnp.exp(log_weight - top)
        total = jnp.sum(factor, axis=0, keepdims=True)
        numer = jnp.zeros((slab, HD), jnp.float32)
        for i in range(n):
            share = parts_ref[i, :, pl.ds(h * HD, HD)].astype(jnp.float32)
            numer = numer + factor[i : i + 1, :].reshape(slab, 1) * share
        columns.append(numer / total.reshape(slab, 1))
    attn = jnp.concatenate(columns, axis=1).astype(jnp.bfloat16)
    out_ref[...] = jnp.dot(attn, w_ref[...], preferred_element_type=jnp.float32).astype(out_ref.dtype)


def _combine_project(parts, log_weight, w_out):
    vmem = pl.BlockSpec(memory_space=pltpu.VMEM)
    return pl.pallas_call(
        _combine_kernel,
        out_shape=jax.ShapeDtypeStruct((parts.shape[1], w_out.shape[1]), jnp.bfloat16),
        in_specs=[vmem] * 3,
        out_specs=vmem,
    )(parts, log_weight, w_out)


def _split_patch(mesh):
    patch = mesh.devices[:, 0]
    sizes = [len({d.coords[k] for d in patch}) for k in range(3)]
    sizes = [n for n in sizes if n > 1]
    if math.prod(sizes) != patch.shape[0] or len(sizes) < 2:
        return mesh, ("patch",)
    names = tuple(f"patch{k}" for k in range(len(sizes)))
    devices = mesh.devices.reshape(*sizes, mesh.devices.shape[1])
    return jax.sharding.Mesh(devices, names + ("head",)), names


PATCH = ("patch",)


def solution(mesh):
    global PATCH
    mesh, PATCH = _split_patch(mesh)
    placed = (
        P((*PATCH, "head"), None),
        P(),
        P(),
        P(),
        P(None, None, "head"),
        P("head", None),
        P("head"),
        P("head"),
        P(None, PATCH, "head"),
    )
    return jax.shard_map(
        per_device,
        mesh=mesh,
        in_specs=placed,
        out_specs=(P((*PATCH, "head"), None), P(None, PATCH, "head")),
        check_vma=False,
    )
```

```python
import math

import jax
import jax.numpy as jnp
from jax import lax
from jax.experimental import pallas as pl
from jax.experimental.pallas import tpu as pltpu
from jax.sharding import PartitionSpec as P

HD = 128


def modulate(x_tokens, shift, scale_mod):
    values_f = x_tokens.astype(jnp.float32)
    center = jnp.mean(values_f, axis=-1, keepdims=True)
    spread = jnp.mean((values_f - center) * (values_f - center), axis=-1, keepdims=True)
    return ((values_f - center) * lax.rsqrt(spread + 1e-06) * (1.0 + scale_mod) + shift).astype(
        jnp.bfloat16
    )


def per_device(x_tokens, shift, scale_mod, gate, w_qkv, w_out, gain_q, gain_k, stale_kv):
    normed = modulate(x_tokens, shift, scale_mod)
    width = w_qkv.shape[1]
    raw = jnp.einsum(
        "nd,cde->cne",
        lax.all_gather(normed, "head", axis=0, tiled=True),
        w_qkv,
        preferred_element_type=jnp.float32,
    )
    squares = jnp.sum(raw[:2] * raw[:2], axis=2)
    squares = jnp.sum(lax.all_gather(squares, "head"), axis=0)
    inverse = lax.rsqrt(squares / width + 1e-06)
    queries = (raw[0] * inverse[0][:, None] * gain_q).astype(jnp.bfloat16)
    keys = (raw[1] * inverse[1][:, None] * gain_k).astype(jnp.bfloat16)
    values = raw[2].astype(jnp.bfloat16)
    fresh_kv = jnp.stack([keys, values])
    parts = _exchange_attention(stale_kv, queries, keys, values)
    own_rows = x_tokens.shape[0]
    groups = queries.shape[0] // own_rows
    whole_terms = _combine_project(parts, w_out)
    pieces = lax.all_to_all(
        whole_terms.reshape(groups, own_rows, whole_terms.shape[1]), "head", 0, 0, tiled=True
    )
    projected = jnp.sum(pieces.astype(jnp.float32), axis=0)
    update = (projected * gate).astype(jnp.bfloat16)
    return (update, fresh_kv)


def _partial_kernel(mask_ref, q_ref, k_ref, v_ref, kv_ref, out_ref):
    queries_n = q_ref.shape[0]
    slab = k_ref.shape[0]
    count = kv_ref.shape[1] // slab
    heads = q_ref.shape[1] // HD
    scale = math.sqrt(HD)
    is_own = mask_ref[...] > 0
    fresh_col = jnp.max(mask_ref[...], axis=0, keepdims=True) > 0
    contract_minor = (((1,), (1,)), ((), ()))
    contract_major = (((0,), (0,)), ((), ()))
    lane = lax.broadcasted_iota(jnp.int32, (queries_n, HD), 1)
    spread = jnp.zeros((queries_n, HD), jnp.float32)
    for h in range(heads):
        cols = pl.ds(h * HD, HD)
        query = q_ref[:, cols]
        scores = lax.dot_general(
            kv_ref[0, :, cols].astype(jnp.bfloat16), query, contract_minor,
            preferred_element_type=jnp.float32,
        ) / scale
        scores = scores.reshape(count, slab, queries_n)
        block_max = jnp.max(scores, axis=1)
        expo = jnp.exp(scores - block_max[:, None, :])
        totals = jnp.sum(expo, axis=1)
        weights = expo.astype(jnp.bfloat16).astype(jnp.float32)
        fresh_scores = lax.dot_general(
            k_ref[:, cols], query, contract_minor, preferred_element_type=jnp.float32
        ) / scale
        fresh_max = jnp.max(fresh_scores, axis=0, keepdims=True)
        fresh_expo = jnp.exp(fresh_scores - fresh_max)
        fresh_total = jnp.sum(fresh_expo, axis=0, keepdims=True)
        fresh_weights = fresh_expo.astype(jnp.bfloat16).astype(jnp.float32)
        top = jnp.max(jnp.where(is_own, -jnp.inf, block_max), axis=0, keepdims=True)
        top = jnp.maximum(top, jnp.where(fresh_col, fresh_max, -jnp.inf))
        factor = jnp.where(is_own, 0.0, jnp.exp(block_max - top))
        fresh_factor = jnp.where(fresh_col, jnp.exp(fresh_max - top), 0.0)
        total = jnp.sum(factor * totals, axis=0, keepdims=True) + fresh_factor * fresh_total
        mixed = (factor[:, None, :] * weights).reshape(count * slab, queries_n)
        numer = lax.dot_general(
            mixed,
            kv_ref[1, :, cols],
            contract_major,
            preferred_element_type=jnp.float32,
            precision=lax.Precision.HIGHEST,
        )
        numer = numer + lax.dot_general(
            fresh_factor * fresh_weights,
            v_ref[:, cols].astype(jnp.float32),
            contract_major,
            preferred_element_type=jnp.float32,
            precision=lax.Precision.HIGHEST,
        )
        out_ref[:, cols] = (numer / total.reshape(queries_n, 1)).astype(out_ref.dtype)
        log_weight = (top + jnp.log(total)).reshape(queries_n, 1)
        spread = jnp.where(lane % 8 == h, log_weight, spread)
    high = spread.astype(jnp.bfloat16).astype(jnp.float32)
    middle = (spread - high).astype(jnp.bfloat16).astype(jnp.float32)
    low = spread - high - middle
    coded = jnp.where(lane < 8, high, jnp.where(lane < 16, middle, jnp.where(lane < 24, low, 0.0)))
    out_ref[:, pl.ds(heads * HD, HD)] = coded.astype(out_ref.dtype)


def _partial_attention(mask, group_queries, keys, values, near_kv):
    vmem = pl.BlockSpec(memory_space=pltpu.VMEM)
    rows, width = group_queries.shape
    return pl.pallas_call(
        _partial_kernel,
        out_shape=jax.ShapeDtypeStruct((rows, width + HD), jnp.bfloat16),
        in_specs=[vmem] * 5,
        out_specs=vmem,
        compiler_params=pltpu.CompilerParams(vmem_limit_bytes=48 * 1024 * 1024),
    )(mask, group_queries, keys, values, near_kv)


def _exchange_attention(stale_kv, queries, keys, values):
    slab, width = queries.shape
    heads = width // HD
    outer, inner = PATCH[:-1], PATCH[-1]
    near_kv = lax.all_gather(stale_kv.astype(jnp.float32), outer, axis=1, tiled=True)
    count = near_kv.shape[1] // slab
    n = lax.psum(1, inner)
    spread = jnp.broadcast_to(queries[None], (n, slab, width)).reshape(n * slab, width)
    group_queries = lax.all_to_all(spread, inner, 0, 0, tiled=True)
    block_ids = jnp.arange(count, dtype=jnp.int32)[:, None]
    slab_ids = (jnp.arange(n * slab, dtype=jnp.int32) // slab)[None, :]
    mask = ((block_ids == lax.axis_index(outer)) & (slab_ids == lax.axis_index(inner))).astype(jnp.int32)
    partial = _partial_attention(mask, group_queries, keys, values, near_kv)
    return lax.all_to_all(partial.reshape(n, slab, width + HD), inner, 0, 0, tiled=True)


def _combine_kernel(parts_ref, w_ref, out_ref):
    n, slab, width = parts_ref.shape
    heads = width // HD - 1
    lane = lax.broadcasted_iota(jnp.int32, (slab, HD), 1)
    coded = [parts_ref[i, :, pl.ds(heads * HD, HD)].astype(jnp.float32) for i in range(n)]
    columns = []
    for h in range(heads):
        pick = (lane % 8 == h) & (lane < 24)
        log_weight = [jnp.sum(jnp.where(pick, c, 0.0), axis=1, keepdims=True) for c in coded]
        top = log_weight[0]
        for w in log_weight[1:]:
            top = jnp.maximum(top, w)
        factor = [jnp.exp(w - top) for w in log_weight]
        total = factor[0]
        for f in factor[1:]:
            total = total + f
        numer = jnp.zeros((slab, HD), jnp.float32)
        for i in range(n):
            numer = numer + factor[i] * parts_ref[i, :, pl.ds(h * HD, HD)].astype(jnp.float32)
        columns.append(numer / total)
    attn = jnp.concatenate(columns, axis=1).astype(jnp.bfloat16)
    out_ref[...] = jnp.dot(attn, w_ref[...], preferred_element_type=jnp.float32).astype(out_ref.dtype)


def _combine_project(parts, w_out):
    vmem = pl.BlockSpec(memory_space=pltpu.VMEM)
    return pl.pallas_call(
        _combine_kernel,
        out_shape=jax.ShapeDtypeStruct((parts.shape[1], w_out.shape[1]), jnp.bfloat16),
        in_specs=[vmem] * 2,
        out_specs=vmem,
    )(parts, w_out)


def _split_patch(mesh):
    patch = mesh.devices[:, 0]
    sizes = [len({d.coords[k] for d in patch}) for k in range(3)]
    sizes = [n for n in sizes if n > 1]
    if math.prod(sizes) != patch.shape[0] or len(sizes) < 2:
        return mesh, ("patch",)
    names = tuple(f"patch{k}" for k in range(len(sizes)))
    devices = mesh.devices.reshape(*sizes, mesh.devices.shape[1])
    return jax.sharding.Mesh(devices, names + ("head",)), names


PATCH = ("patch",)


def solution(mesh):
    global PATCH
    mesh, PATCH = _split_patch(mesh)
    placed = (
        P((*PATCH, "head"), None),
        P(),
        P(),
        P(),
        P(None, None, "head"),
        P("head", None),
        P("head"),
        P("head"),
        P(None, PATCH, "head"),
    )
    return jax.shard_map(
        per_device,
        mesh=mesh,
        in_specs=placed,
        out_specs=(P((*PATCH, "head"), None), P(None, PATCH, "head")),
        check_vma=False,
    )
```

```python
import math

import jax
import jax.numpy as jnp
from jax import lax
from jax.experimental import pallas as pl
from jax.experimental.pallas import tpu as pltpu
from jax.sharding import PartitionSpec as P

HD = 128


def modulate(x_tokens, shift, scale_mod):
    values_f = x_tokens.astype(jnp.float32)
    center = jnp.mean(values_f, axis=-1, keepdims=True)
    spread = jnp.mean((values_f - center) * (values_f - center), axis=-1, keepdims=True)
    return ((values_f - center) * lax.rsqrt(spread + 1e-06) * (1.0 + scale_mod) + shift).astype(
        jnp.bfloat16
    )


def per_device(x_tokens, shift, scale_mod, gate, w_qkv, w_out, gain_q, gain_k, stale_kv):
    near_kv = _ring(stale_kv, PATCH[-2])
    normed = modulate(x_tokens, shift, scale_mod)
    width = w_qkv.shape[1]
    raw = jnp.einsum(
        "nd,cde->cne",
        lax.all_gather(normed, "head", axis=0, tiled=True),
        w_qkv,
        preferred_element_type=jnp.float32,
    )
    squares = jnp.sum(raw[:2] * raw[:2], axis=2)
    near_kv, squares = lax.optimization_barrier((near_kv, squares))
    squares = jnp.sum(lax.all_gather(squares, "head"), axis=0)
    for name in reversed(PATCH[:-2]):
        near_kv = _ring(near_kv, name)
    inverse = lax.rsqrt(squares / width + 1e-06)
    queries = (raw[0] * inverse[0][:, None] * gain_q).astype(jnp.bfloat16)
    keys = (raw[1] * inverse[1][:, None] * gain_k).astype(jnp.bfloat16)
    values = raw[2].astype(jnp.bfloat16)
    fresh_kv = jnp.stack([keys, values])
    parts = _exchange_attention(near_kv, queries, keys, values)
    own_rows = x_tokens.shape[0]
    groups = queries.shape[0] // own_rows
    whole_terms = _combine_project(parts, w_out)
    pieces = lax.all_to_all(
        whole_terms.reshape(groups, own_rows, whole_terms.shape[1]), "head", 0, 0, tiled=True
    )
    projected = jnp.sum(pieces.astype(jnp.float32), axis=0)
    update = (projected * gate).astype(jnp.bfloat16)
    return (update, fresh_kv)


def _partial_kernel(mask_ref, q_ref, k_ref, v_ref, kv_ref, out_ref):
    queries_n = q_ref.shape[0]
    slab = k_ref.shape[0]
    count = kv_ref.shape[1] // slab
    heads = q_ref.shape[1] // HD
    scale = math.sqrt(HD)
    is_own = mask_ref[...] > 0
    fresh_col = jnp.max(mask_ref[...], axis=0, keepdims=True) > 0
    contract_minor = (((1,), (1,)), ((), ()))
    contract_major = (((0,), (0,)), ((), ()))
    lane = lax.broadcasted_iota(jnp.int32, (queries_n, HD), 1)
    spread = jnp.zeros((queries_n, HD), jnp.float32)
    for h in range(heads):
        cols = pl.ds(h * HD, HD)
        query = q_ref[:, cols]
        scores = lax.dot_general(
            kv_ref[0, :, cols], query, contract_minor,
            preferred_element_type=jnp.float32,
        ) / scale
        scores = scores.reshape(count, slab, queries_n)
        block_max = jnp.max(scores, axis=1)
        expo = jnp.exp(scores - block_max[:, None, :])
        totals = jnp.sum(expo, axis=1)
        weights = expo.astype(jnp.bfloat16).astype(jnp.float32)
        fresh_scores = lax.dot_general(
            k_ref[:, cols], query, contract_minor, preferred_element_type=jnp.float32
        ) / scale
        fresh_max = jnp.max(fresh_scores, axis=0, keepdims=True)
        fresh_expo = jnp.exp(fresh_scores - fresh_max)
        fresh_total = jnp.sum(fresh_expo, axis=0, keepdims=True)
        fresh_weights = fresh_expo.astype(jnp.bfloat16).astype(jnp.float32)
        top = jnp.max(jnp.where(is_own, -jnp.inf, block_max), axis=0, keepdims=True)
        top = jnp.maximum(top, jnp.where(fresh_col, fresh_max, -jnp.inf))
        factor = jnp.where(is_own, 0.0, jnp.exp(block_max - top))
        fresh_factor = jnp.where(fresh_col, jnp.exp(fresh_max - top), 0.0)
        total = jnp.sum(factor * totals, axis=0, keepdims=True) + fresh_factor * fresh_total
        mixed = (factor[:, None, :] * weights).reshape(count * slab, queries_n)
        numer = lax.dot_general(
            mixed,
            kv_ref[1, :, cols].astype(jnp.float32),
            contract_major,
            preferred_element_type=jnp.float32,
            precision=lax.Precision.HIGHEST,
        )
        numer = numer + lax.dot_general(
            fresh_factor * fresh_weights,
            v_ref[:, cols].astype(jnp.float32),
            contract_major,
            preferred_element_type=jnp.float32,
            precision=lax.Precision.HIGHEST,
        )
        out_ref[:, cols] = (numer / total.reshape(queries_n, 1)).astype(out_ref.dtype)
        log_weight = (top + jnp.log(total)).reshape(queries_n, 1)
        spread = jnp.where(lane % 8 == h, log_weight, spread)
    high = spread.astype(jnp.bfloat16).astype(jnp.float32)
    middle = (spread - high).astype(jnp.bfloat16).astype(jnp.float32)
    low = spread - high - middle
    coded = jnp.where(lane < 8, high, jnp.where(lane < 16, middle, jnp.where(lane < 24, low, 0.0)))
    out_ref[:, pl.ds(heads * HD, HD)] = coded.astype(out_ref.dtype)


def _partial_attention(mask, group_queries, keys, values, near_kv):
    vmem = pl.BlockSpec(memory_space=pltpu.VMEM)
    rows, width = group_queries.shape
    return pl.pallas_call(
        _partial_kernel,
        out_shape=jax.ShapeDtypeStruct((rows, width + HD), jnp.bfloat16),
        in_specs=[vmem] * 5,
        out_specs=vmem,
        compiler_params=pltpu.CompilerParams(vmem_limit_bytes=48 * 1024 * 1024),
    )(mask, group_queries, keys, values, near_kv)


def _ring(blocks, name):
    size = lax.psum(1, name)
    parts = [blocks]
    for shift in range(1, size):
        pairs = [(src, (src + shift) % size) for src in range(size)]
        parts.append(lax.ppermute(blocks, name, pairs))
    return jnp.concatenate(parts, axis=1)


def _exchange_attention(near_kv, queries, keys, values):
    slab, width = queries.shape
    heads = width // HD
    outer, inner = PATCH[:-1], PATCH[-1]
    count = near_kv.shape[1] // slab
    n = lax.psum(1, inner)
    spread = jnp.broadcast_to(queries[None], (n, slab, width)).reshape(n * slab, width)
    group_queries = lax.all_to_all(spread, inner, 0, 0, tiled=True)
    block_ids = jnp.arange(count, dtype=jnp.int32)[:, None]
    slab_ids = (jnp.arange(n * slab, dtype=jnp.int32) // slab)[None, :]
    mask = ((block_ids == 0) & (slab_ids == lax.axis_index(inner))).astype(jnp.int32)
    partial = _partial_attention(mask, group_queries, keys, values, near_kv)
    return lax.all_to_all(partial.reshape(n, slab, width + HD), inner, 0, 0, tiled=True)


def _combine_kernel(parts_ref, w_ref, out_ref):
    n, slab, width = parts_ref.shape
    heads = width // HD - 1
    lane = lax.broadcasted_iota(jnp.int32, (slab, HD), 1)
    coded = [parts_ref[i, :, pl.ds(heads * HD, HD)].astype(jnp.float32) for i in range(n)]
    columns = []
    for h in range(heads):
        pick = (lane % 8 == h) & (lane < 24)
        log_weight = [jnp.sum(jnp.where(pick, c, 0.0), axis=1, keepdims=True) for c in coded]
        top = log_weight[0]
        for w in log_weight[1:]:
            top = jnp.maximum(top, w)
        factor = [jnp.exp(w - top) for w in log_weight]
        total = factor[0]
        for f in factor[1:]:
            total = total + f
        numer = jnp.zeros((slab, HD), jnp.float32)
        for i in range(n):
            numer = numer + factor[i] * parts_ref[i, :, pl.ds(h * HD, HD)].astype(jnp.float32)
        columns.append(numer / total)
    attn = jnp.concatenate(columns, axis=1).astype(jnp.bfloat16)
    out_ref[...] = jnp.dot(attn, w_ref[...], preferred_element_type=jnp.float32).astype(out_ref.dtype)


def _combine_project(parts, w_out):
    vmem = pl.BlockSpec(memory_space=pltpu.VMEM)
    return pl.pallas_call(
        _combine_kernel,
        out_shape=jax.ShapeDtypeStruct((parts.shape[1], w_out.shape[1]), jnp.bfloat16),
        in_specs=[vmem] * 2,
        out_specs=vmem,
    )(parts, w_out)


def _split_patch(mesh):
    patch = mesh.devices[:, 0]
    sizes = [len({d.coords[k] for d in patch}) for k in range(3)]
    sizes = [n for n in sizes if n > 1]
    if math.prod(sizes) != patch.shape[0] or len(sizes) < 2:
        return mesh, ("patch",)
    names = tuple(f"patch{k}" for k in range(len(sizes)))
    devices = mesh.devices.reshape(*sizes, mesh.devices.shape[1])
    return jax.sharding.Mesh(devices, names + ("head",)), names


PATCH = ("patch",)


def solution(mesh):
    global PATCH
    mesh, PATCH = _split_patch(mesh)
    placed = (
        P((*PATCH, "head"), None),
        P(),
        P(),
        P(),
        P(None, None, "head"),
        P("head", None),
        P("head"),
        P("head"),
        P(None, PATCH, "head"),
    )
    return jax.shard_map(
        per_device,
        mesh=mesh,
        in_specs=placed,
        out_specs=(P((*PATCH, "head"), None), P(None, PATCH, "head")),
        check_vma=False,
    )
```

```python
import math

import jax
import jax.numpy as jnp
from jax import lax
from jax.experimental import pallas as pl
from jax.experimental.pallas import tpu as pltpu
from jax.sharding import PartitionSpec as P

HD = 128


def modulate(x_tokens, shift, scale_mod):
    values_f = x_tokens.astype(jnp.float32)
    center = jnp.mean(values_f, axis=-1, keepdims=True)
    spread = jnp.mean((values_f - center) * (values_f - center), axis=-1, keepdims=True)
    return ((values_f - center) * lax.rsqrt(spread + 1e-06) * (1.0 + scale_mod) + shift).astype(
        jnp.bfloat16
    )


def per_device(x_tokens, shift, scale_mod, gate, w_qkv, w_out, gain_q, gain_k, stale_kv):
    normed = modulate(x_tokens, shift, scale_mod)
    width = w_qkv.shape[1]
    raw = jnp.einsum(
        "nd,cde->cne",
        lax.all_gather(normed, "head", axis=0, tiled=True),
        w_qkv,
        preferred_element_type=jnp.float32,
    )
    squares = jnp.sum(raw[:2] * raw[:2], axis=2)
    squares = jnp.sum(lax.all_gather(squares, "head"), axis=0)
    inverse = lax.rsqrt(squares / width + 1e-06)
    queries = (raw[0] * inverse[0][:, None] * gain_q).astype(jnp.bfloat16)
    keys = (raw[1] * inverse[1][:, None] * gain_k).astype(jnp.bfloat16)
    values = raw[2].astype(jnp.bfloat16)
    fresh_kv = jnp.stack([keys, values])
    parts = _exchange_attention(stale_kv, queries, keys, values)
    own_rows = x_tokens.shape[0]
    groups = queries.shape[0] // own_rows
    whole_terms = _combine_project(parts, w_out)
    pieces = lax.all_to_all(
        whole_terms.reshape(groups, own_rows, whole_terms.shape[1]), "head", 0, 0, tiled=True
    )
    projected = jnp.sum(pieces.astype(jnp.float32), axis=0)
    update = (projected * gate).astype(jnp.bfloat16)
    return (update, fresh_kv)


def _partial_kernel(mask_ref, q_ref, k_ref, v_ref, kv_ref, out_ref):
    queries_n = q_ref.shape[0]
    slab = k_ref.shape[0]
    count = kv_ref.shape[1] // slab
    heads = q_ref.shape[1] // HD
    scale = math.sqrt(HD)
    is_own = mask_ref[...] > 0
    fresh_col = jnp.max(mask_ref[...], axis=0, keepdims=True) > 0
    contract_minor = (((1,), (1,)), ((), ()))
    contract_major = (((0,), (0,)), ((), ()))
    lane = lax.broadcasted_iota(jnp.int32, (queries_n, HD), 1)
    spread = jnp.zeros((queries_n, HD), jnp.float32)
    for h in range(heads):
        cols = pl.ds(h * HD, HD)
        query = q_ref[:, cols]
        scores = lax.dot_general(
            kv_ref[0, :, cols], query, contract_minor,
            preferred_element_type=jnp.float32,
        ) / scale
        scores = scores.reshape(count, slab, queries_n)
        block_max = jnp.max(scores, axis=1)
        expo = jnp.exp(scores - block_max[:, None, :])
        totals = jnp.sum(expo, axis=1)
        weights = expo.astype(jnp.bfloat16).astype(jnp.float32)
        fresh_scores = lax.dot_general(
            k_ref[:, cols], query, contract_minor, preferred_element_type=jnp.float32
        ) / scale
        fresh_max = jnp.max(fresh_scores, axis=0, keepdims=True)
        fresh_expo = jnp.exp(fresh_scores - fresh_max)
        fresh_total = jnp.sum(fresh_expo, axis=0, keepdims=True)
        fresh_weights = fresh_expo.astype(jnp.bfloat16).astype(jnp.float32)
        top = jnp.max(jnp.where(is_own, -jnp.inf, block_max), axis=0, keepdims=True)
        top = jnp.maximum(top, jnp.where(fresh_col, fresh_max, -jnp.inf))
        factor = jnp.where(is_own, 0.0, jnp.exp(block_max - top))
        fresh_factor = jnp.where(fresh_col, jnp.exp(fresh_max - top), 0.0)
        total = jnp.sum(factor * totals, axis=0, keepdims=True) + fresh_factor * fresh_total
        mixed = (factor[:, None, :] * weights).reshape(count * slab, queries_n)
        numer = lax.dot_general(
            mixed,
            kv_ref[1, :, cols].astype(jnp.float32),
            contract_major,
            preferred_element_type=jnp.float32,
            precision=lax.Precision.HIGHEST,
        )
        numer = numer + lax.dot_general(
            fresh_factor * fresh_weights,
            v_ref[:, cols].astype(jnp.float32),
            contract_major,
            preferred_element_type=jnp.float32,
            precision=lax.Precision.HIGHEST,
        )
        out_ref[:, cols] = (numer / total.reshape(queries_n, 1)).astype(out_ref.dtype)
        log_weight = (top + jnp.log(total)).reshape(queries_n, 1)
        spread = jnp.where(lane % 8 == h, log_weight, spread)
    high = spread.astype(jnp.bfloat16).astype(jnp.float32)
    middle = (spread - high).astype(jnp.bfloat16).astype(jnp.float32)
    low = spread - high - middle
    coded = jnp.where(lane < 8, high, jnp.where(lane < 16, middle, jnp.where(lane < 24, low, 0.0)))
    out_ref[:, pl.ds(heads * HD, HD)] = coded.astype(out_ref.dtype)


def _partial_attention(mask, group_queries, keys, values, near_kv):
    vmem = pl.BlockSpec(memory_space=pltpu.VMEM)
    rows, width = group_queries.shape
    return pl.pallas_call(
        _partial_kernel,
        out_shape=jax.ShapeDtypeStruct((rows, width + HD), jnp.bfloat16),
        in_specs=[vmem] * 5,
        out_specs=vmem,
        compiler_params=pltpu.CompilerParams(vmem_limit_bytes=48 * 1024 * 1024),
    )(mask, group_queries, keys, values, near_kv)


def _exchange_attention(stale_kv, queries, keys, values):
    slab, width = queries.shape
    heads = width // HD
    outer, inner = PATCH[:-1], PATCH[-1]
    m = math.prod(lax.psum(1, name) for name in outer)
    spread_kv = jnp.broadcast_to(stale_kv[:, None], (2, m) + stale_kv.shape[1:])
    near_kv = lax.all_to_all(spread_kv.reshape(2, m * slab, width), outer, 1, 1, tiled=True)
    count = near_kv.shape[1] // slab
    n = lax.psum(1, inner)
    spread = jnp.broadcast_to(queries[None], (n, slab, width)).reshape(n * slab, width)
    group_queries = lax.all_to_all(spread, inner, 0, 0, tiled=True)
    block_ids = jnp.arange(count, dtype=jnp.int32)[:, None]
    slab_ids = (jnp.arange(n * slab, dtype=jnp.int32) // slab)[None, :]
    mask = ((block_ids == lax.axis_index(outer)) & (slab_ids == lax.axis_index(inner))).astype(jnp.int32)
    partial = _partial_attention(mask, group_queries, keys, values, near_kv)
    return lax.all_to_all(partial.reshape(n, slab, width + HD), inner, 0, 0, tiled=True)


def _combine_kernel(parts_ref, w_ref, out_ref):
    n, slab, width = parts_ref.shape
    heads = width // HD - 1
    lane = lax.broadcasted_iota(jnp.int32, (slab, HD), 1)
    coded = [parts_ref[i, :, pl.ds(heads * HD, HD)].astype(jnp.float32) for i in range(n)]
    columns = []
    for h in range(heads):
        pick = (lane % 8 == h) & (lane < 24)
        log_weight = [jnp.sum(jnp.where(pick, c, 0.0), axis=1, keepdims=True) for c in coded]
        top = log_weight[0]
        for w in log_weight[1:]:
            top = jnp.maximum(top, w)
        factor = [jnp.exp(w - top) for w in log_weight]
        total = factor[0]
        for f in factor[1:]:
            total = total + f
        numer = jnp.zeros((slab, HD), jnp.float32)
        for i in range(n):
            numer = numer + factor[i] * parts_ref[i, :, pl.ds(h * HD, HD)].astype(jnp.float32)
        columns.append(numer / total)
    attn = jnp.concatenate(columns, axis=1).astype(jnp.bfloat16)
    out_ref[...] = jnp.dot(attn, w_ref[...], preferred_element_type=jnp.float32).astype(out_ref.dtype)


def _combine_project(parts, w_out):
    vmem = pl.BlockSpec(memory_space=pltpu.VMEM)
    return pl.pallas_call(
        _combine_kernel,
        out_shape=jax.ShapeDtypeStruct((parts.shape[1], w_out.shape[1]), jnp.bfloat16),
        in_specs=[vmem] * 2,
        out_specs=vmem,
    )(parts, w_out)


def _split_patch(mesh):
    patch = mesh.devices[:, 0]
    sizes = [len({d.coords[k] for d in patch}) for k in range(3)]
    sizes = [n for n in sizes if n > 1]
    if math.prod(sizes) != patch.shape[0] or len(sizes) < 2:
        return mesh, ("patch",)
    names = tuple(f"patch{k}" for k in range(len(sizes)))
    devices = mesh.devices.reshape(*sizes, mesh.devices.shape[1])
    return jax.sharding.Mesh(devices, names + ("head",)), names


PATCH = ("patch",)


def solution(mesh):
    global PATCH
    mesh, PATCH = _split_patch(mesh)
    placed = (
        P((*PATCH, "head"), None),
        P(),
        P(),
        P(),
        P(None, None, "head"),
        P("head", None),
        P("head"),
        P("head"),
        P(None, PATCH, "head"),
    )
    return jax.shard_map(
        per_device,
        mesh=mesh,
        in_specs=placed,
        out_specs=(P((*PATCH, "head"), None), P(None, PATCH, "head")),
        check_vma=False,
    )
```

```python
import math

import jax
import jax.numpy as jnp
from jax import lax
from jax.experimental import pallas as pl
from jax.experimental.pallas import tpu as pltpu
from jax.sharding import PartitionSpec as P

HD = 128


def modulate(x_tokens, shift, scale_mod):
    values_f = x_tokens.astype(jnp.float32)
    center = jnp.mean(values_f, axis=-1, keepdims=True)
    spread = jnp.mean((values_f - center) * (values_f - center), axis=-1, keepdims=True)
    return ((values_f - center) * lax.rsqrt(spread + 1e-06) * (1.0 + scale_mod) + shift).astype(
        jnp.bfloat16
    )


def per_device(x_tokens, shift, scale_mod, gate, w_qkv, w_out, gain_q, gain_k, stale_kv):
    normed = modulate(x_tokens, shift, scale_mod)
    width = w_qkv.shape[1]
    raw = jnp.einsum(
        "nd,cde->cne",
        lax.all_gather(normed, "head", axis=0, tiled=True),
        w_qkv,
        preferred_element_type=jnp.float32,
    )
    squares = jnp.sum(raw[:2] * raw[:2], axis=2)
    squares = jnp.sum(lax.all_gather(squares, "head"), axis=0)
    inverse = lax.rsqrt(squares / width + 1e-06)
    queries = (raw[0] * inverse[0][:, None] * gain_q).astype(jnp.bfloat16)
    keys = (raw[1] * inverse[1][:, None] * gain_k).astype(jnp.bfloat16)
    values = raw[2].astype(jnp.bfloat16)
    fresh_kv = jnp.stack([keys, values])
    parts = _exchange_attention(stale_kv, queries, keys, values)
    own_rows = x_tokens.shape[0]
    groups = queries.shape[0] // own_rows
    whole_terms = _combine_project(parts, w_out)
    pieces = lax.all_to_all(
        whole_terms.reshape(groups, own_rows, whole_terms.shape[1]), "head", 0, 0, tiled=True
    )
    projected = jnp.sum(pieces.astype(jnp.float32), axis=0)
    update = (projected * gate).astype(jnp.bfloat16)
    return (update, fresh_kv)


def _partial_kernel(mask_ref, q_ref, k_ref, v_ref, kv_ref, out_ref):
    queries_n = q_ref.shape[0]
    slab = k_ref.shape[0]
    count = kv_ref.shape[1] // slab
    heads = q_ref.shape[1] // HD
    scale = math.sqrt(HD)
    is_own = mask_ref[...] > 0
    fresh_col = jnp.max(mask_ref[...], axis=0, keepdims=True) > 0
    contract_minor = (((1,), (1,)), ((), ()))
    contract_major = (((0,), (0,)), ((), ()))
    lane = lax.broadcasted_iota(jnp.int32, (queries_n, HD), 1)
    spread = jnp.zeros((queries_n, HD), jnp.float32)
    for h in range(heads):
        cols = pl.ds(h * HD, HD)
        query = q_ref[:, cols]
        scores = lax.dot_general(
            kv_ref[0, :, cols], query, contract_minor,
            preferred_element_type=jnp.float32,
        ) / scale
        scores = scores.reshape(count, slab, queries_n)
        block_max = jnp.max(scores, axis=1)
        expo = jnp.exp(scores - block_max[:, None, :])
        totals = jnp.sum(expo, axis=1)
        weights = expo.astype(jnp.bfloat16).astype(jnp.float32)
        fresh_scores = lax.dot_general(
            k_ref[:, cols], query, contract_minor, preferred_element_type=jnp.float32
        ) / scale
        fresh_max = jnp.max(fresh_scores, axis=0, keepdims=True)
        fresh_expo = jnp.exp(fresh_scores - fresh_max)
        fresh_total = jnp.sum(fresh_expo, axis=0, keepdims=True)
        fresh_weights = fresh_expo.astype(jnp.bfloat16).astype(jnp.float32)
        top = jnp.max(jnp.where(is_own, -jnp.inf, block_max), axis=0, keepdims=True)
        top = jnp.maximum(top, jnp.where(fresh_col, fresh_max, -jnp.inf))
        factor = jnp.where(is_own, 0.0, jnp.exp(block_max - top))
        fresh_factor = jnp.where(fresh_col, jnp.exp(fresh_max - top), 0.0)
        total = jnp.sum(factor * totals, axis=0, keepdims=True) + fresh_factor * fresh_total
        mixed = (factor[:, None, :] * weights).reshape(count * slab, queries_n)
        numer = lax.dot_general(
            mixed,
            kv_ref[1, :, cols].astype(jnp.float32),
            contract_major,
            preferred_element_type=jnp.float32,
            precision=lax.Precision.HIGHEST,
        )
        numer = numer + lax.dot_general(
            fresh_factor * fresh_weights,
            v_ref[:, cols].astype(jnp.float32),
            contract_major,
            preferred_element_type=jnp.float32,
            precision=lax.Precision.HIGHEST,
        )
        out_ref[:, cols] = (numer / total.reshape(queries_n, 1)).astype(out_ref.dtype)
        log_weight = (top + jnp.log(total)).reshape(queries_n, 1)
        spread = jnp.where(lane % 8 == h, log_weight, spread)
    high = spread.astype(jnp.bfloat16).astype(jnp.float32)
    middle = (spread - high).astype(jnp.bfloat16).astype(jnp.float32)
    low = spread - high - middle
    coded = jnp.where(lane < 8, high, jnp.where(lane < 16, middle, jnp.where(lane < 24, low, 0.0)))
    out_ref[:, pl.ds(heads * HD, HD)] = coded.astype(out_ref.dtype)


def _partial_attention(mask, group_queries, keys, values, near_kv):
    vmem = pl.BlockSpec(memory_space=pltpu.VMEM)
    rows, width = group_queries.shape
    return pl.pallas_call(
        _partial_kernel,
        out_shape=jax.ShapeDtypeStruct((rows, width + HD), jnp.bfloat16),
        in_specs=[vmem] * 5,
        out_specs=vmem,
        compiler_params=pltpu.CompilerParams(vmem_limit_bytes=48 * 1024 * 1024),
    )(mask, group_queries, keys, values, near_kv)


def _exchange_attention(stale_kv, queries, keys, values):
    slab, width = queries.shape
    kv_axes, q_axes = PATCH[-1:], PATCH[:-1]
    m = math.prod(lax.psum(1, name) for name in kv_axes)
    spread_kv = jnp.broadcast_to(stale_kv[:, None], (2, m) + stale_kv.shape[1:])
    near_kv = lax.all_to_all(spread_kv.reshape(2, m * slab, width), kv_axes, 1, 1, tiled=True)
    count = near_kv.shape[1] // slab
    n = math.prod(lax.psum(1, name) for name in q_axes)
    spread = jnp.broadcast_to(queries[None], (n, slab, width)).reshape(n * slab, width)
    group_queries = lax.all_to_all(spread, q_axes, 0, 0, tiled=True)
    block_ids = jnp.arange(count, dtype=jnp.int32)[:, None]
    slab_ids = (jnp.arange(n * slab, dtype=jnp.int32) // slab)[None, :]
    mask = (block_ids == lax.axis_index(kv_axes)) & (slab_ids == lax.axis_index(q_axes))
    partial = _partial_attention(mask.astype(jnp.int32), group_queries, keys, values, near_kv)
    return lax.all_to_all(partial.reshape(n, slab, width + HD), q_axes, 0, 0, tiled=True)


def _combine_kernel(parts_ref, w_ref, out_ref):
    n, slab, width = parts_ref.shape
    heads = width // HD - 1
    lane = lax.broadcasted_iota(jnp.int32, (slab, HD), 1)
    coded = [parts_ref[i, :, pl.ds(heads * HD, HD)].astype(jnp.float32) for i in range(n)]
    columns = []
    for h in range(heads):
        pick = (lane % 8 == h) & (lane < 24)
        log_weight = [jnp.sum(jnp.where(pick, c, 0.0), axis=1, keepdims=True) for c in coded]
        top = log_weight[0]
        for w in log_weight[1:]:
            top = jnp.maximum(top, w)
        factor = [jnp.exp(w - top) for w in log_weight]
        total = factor[0]
        for f in factor[1:]:
            total = total + f
        numer = jnp.zeros((slab, HD), jnp.float32)
        for i in range(n):
            numer = numer + factor[i] * parts_ref[i, :, pl.ds(h * HD, HD)].astype(jnp.float32)
        columns.append(numer / total)
    attn = jnp.concatenate(columns, axis=1).astype(jnp.bfloat16)
    out_ref[...] = jnp.dot(attn, w_ref[...], preferred_element_type=jnp.float32).astype(out_ref.dtype)


def _combine_project(parts, w_out):
    vmem = pl.BlockSpec(memory_space=pltpu.VMEM)
    return pl.pallas_call(
        _combine_kernel,
        out_shape=jax.ShapeDtypeStruct((parts.shape[1], w_out.shape[1]), jnp.bfloat16),
        in_specs=[vmem] * 2,
        out_specs=vmem,
    )(parts, w_out)


def _split_patch(mesh):
    patch = mesh.devices[:, 0]
    sizes = [len({d.coords[k] for d in patch}) for k in range(3)]
    sizes = [n for n in sizes if n > 1]
    if math.prod(sizes) != patch.shape[0] or len(sizes) < 2:
        return mesh, ("patch",)
    names = tuple(f"patch{k}" for k in range(len(sizes)))
    devices = mesh.devices.reshape(*sizes, mesh.devices.shape[1])
    return jax.sharding.Mesh(devices, names + ("head",)), names


PATCH = ("patch",)


def solution(mesh):
    global PATCH
    mesh, PATCH = _split_patch(mesh)
    placed = (
        P((*PATCH, "head"), None),
        P(),
        P(),
        P(),
        P(None, None, "head"),
        P("head", None),
        P("head"),
        P("head"),
        P(None, PATCH, "head"),
    )
    return jax.shard_map(
        per_device,
        mesh=mesh,
        in_specs=placed,
        out_specs=(P((*PATCH, "head"), None), P(None, PATCH, "head")),
        check_vma=False,
    )
```

```python
import math

import jax
import jax.numpy as jnp
from jax import lax
from jax.experimental import pallas as pl
from jax.experimental.pallas import tpu as pltpu
from jax.sharding import PartitionSpec as P

HD = 128


def modulate(x_tokens, shift, scale_mod):
    values_f = x_tokens.astype(jnp.float32)
    center = jnp.mean(values_f, axis=-1, keepdims=True)
    spread = jnp.mean((values_f - center) * (values_f - center), axis=-1, keepdims=True)
    return ((values_f - center) * lax.rsqrt(spread + 1e-06) * (1.0 + scale_mod) + shift).astype(
        jnp.bfloat16
    )


def per_device(x_tokens, shift, scale_mod, gate, w_qkv, w_out, gain_q, gain_k, stale_kv):
    normed = modulate(x_tokens, shift, scale_mod)
    width = w_qkv.shape[1]
    raw = jnp.einsum(
        "nd,cde->cne",
        lax.all_gather(normed, "head", axis=0, tiled=True),
        w_qkv,
        preferred_element_type=jnp.float32,
    )
    squares = jnp.sum(raw[:2] * raw[:2], axis=2)
    squares = jnp.sum(lax.all_gather(squares, "head"), axis=0)
    inverse = lax.rsqrt(squares / width + 1e-06)
    queries = (raw[0] * inverse[0][:, None] * gain_q).astype(jnp.bfloat16)
    keys = (raw[1] * inverse[1][:, None] * gain_k).astype(jnp.bfloat16)
    values = raw[2].astype(jnp.bfloat16)
    fresh_kv = jnp.stack([keys, values])
    parts = _exchange_attention(stale_kv, queries, keys, values)
    own_rows = x_tokens.shape[0]
    groups = queries.shape[0] // own_rows
    whole_terms = _combine_project(parts, w_out)
    pieces = lax.all_to_all(
        whole_terms.reshape(groups, own_rows, whole_terms.shape[1]), "head", 0, 0, tiled=True
    )
    projected = jnp.sum(pieces.astype(jnp.float32), axis=0)
    update = (projected * gate).astype(jnp.bfloat16)
    return (update, fresh_kv)


def _partial_kernel(own_ref, q_ref, k_ref, v_ref, kv_ref, out_ref):
    queries_n = q_ref.shape[0]
    slab = k_ref.shape[0]
    count = kv_ref.shape[0]
    heads = q_ref.shape[1] // HD
    scale = math.sqrt(HD)
    query_slab = lax.broadcasted_iota(jnp.int32, (1, queries_n), 1) // slab
    fresh_col = query_slab == own_ref[1]
    is_own = (lax.broadcasted_iota(jnp.int32, (count, queries_n), 0) == own_ref[0]) & fresh_col
    contract_minor = (((1,), (1,)), ((), ()))
    contract_major = (((0,), (0,)), ((), ()))
    lane = lax.broadcasted_iota(jnp.int32, (queries_n, HD), 1)
    spread = jnp.zeros((queries_n, HD), jnp.float32)
    for h in range(heads):
        cols = pl.ds(h * HD, HD)
        query = q_ref[:, cols]
        scores = lax.dot_general(
            kv_ref[:, pl.ds(0, slab), cols].reshape(count * slab, HD), query, contract_minor,
            preferred_element_type=jnp.float32,
        ) / scale
        scores = scores.reshape(count, slab, queries_n)
        block_max = jnp.max(scores, axis=1)
        expo = jnp.exp(scores - block_max[:, None, :])
        totals = jnp.sum(expo, axis=1)
        weights = expo.astype(jnp.bfloat16).astype(jnp.float32)
        fresh_scores = lax.dot_general(
            k_ref[:, cols], query, contract_minor, preferred_element_type=jnp.float32
        ) / scale
        fresh_max = jnp.max(fresh_scores, axis=0, keepdims=True)
        fresh_expo = jnp.exp(fresh_scores - fresh_max)
        fresh_total = jnp.sum(fresh_expo, axis=0, keepdims=True)
        fresh_weights = fresh_expo.astype(jnp.bfloat16).astype(jnp.float32)
        top = jnp.max(jnp.where(is_own, -jnp.inf, block_max), axis=0, keepdims=True)
        top = jnp.maximum(top, jnp.where(fresh_col, fresh_max, -jnp.inf))
        factor = jnp.where(is_own, 0.0, jnp.exp(block_max - top))
        fresh_factor = jnp.where(fresh_col, jnp.exp(fresh_max - top), 0.0)
        total = jnp.sum(factor * totals, axis=0, keepdims=True) + fresh_factor * fresh_total
        mixed = (factor[:, None, :] * weights).reshape(count * slab, queries_n)
        numer = lax.dot_general(
            mixed,
            kv_ref[:, pl.ds(slab, slab), cols].reshape(count * slab, HD).astype(jnp.float32),
            contract_major,
            preferred_element_type=jnp.float32,
            precision=lax.Precision.HIGHEST,
        )
        numer = numer + lax.dot_general(
            fresh_factor * fresh_weights,
            v_ref[:, cols].astype(jnp.float32),
            contract_major,
            preferred_element_type=jnp.float32,
            precision=lax.Precision.HIGHEST,
        )
        out_ref[:, cols] = (numer / total.reshape(queries_n, 1)).astype(out_ref.dtype)
        log_weight = (top + jnp.log(total)).reshape(queries_n, 1)
        spread = jnp.where(lane % 8 == h, log_weight, spread)
    high = spread.astype(jnp.bfloat16).astype(jnp.float32)
    middle = (spread - high).astype(jnp.bfloat16).astype(jnp.float32)
    low = spread - high - middle
    coded = jnp.where(lane < 8, high, jnp.where(lane < 16, middle, jnp.where(lane < 24, low, 0.0)))
    out_ref[:, pl.ds(heads * HD, HD)] = coded.astype(out_ref.dtype)


def _partial_attention(own, group_queries, keys, values, near_kv):
    vmem = pl.BlockSpec(memory_space=pltpu.VMEM)
    smem = pl.BlockSpec(memory_space=pltpu.SMEM)
    rows, width = group_queries.shape
    return pl.pallas_call(
        _partial_kernel,
        out_shape=jax.ShapeDtypeStruct((rows, width + HD), jnp.bfloat16),
        in_specs=[smem] + [vmem] * 4,
        out_specs=vmem,
        compiler_params=pltpu.CompilerParams(vmem_limit_bytes=48 * 1024 * 1024),
    )(own, group_queries, keys, values, near_kv)


def _exchange_attention(stale_kv, queries, keys, values):
    slab, width = queries.shape
    kv_axes, q_axes = PATCH[-1:], PATCH[:-1]
    m = math.prod(lax.psum(1, name) for name in kv_axes)
    rows = stale_kv.reshape(2 * slab, width)
    spread_kv = jnp.broadcast_to(rows[None], (m, 2 * slab, width))
    near_kv = lax.all_to_all(spread_kv, kv_axes, 0, 0, tiled=True)
    n = math.prod(lax.psum(1, name) for name in q_axes)
    spread = jnp.broadcast_to(queries[None], (n, slab, width)).reshape(n * slab, width)
    group_queries = lax.all_to_all(spread, q_axes, 0, 0, tiled=True)
    own = jnp.stack([lax.axis_index(kv_axes), lax.axis_index(q_axes)]).astype(jnp.int32)
    partial = _partial_attention(own, group_queries, keys, values, near_kv)
    return lax.all_to_all(partial.reshape(n, slab, width + HD), q_axes, 0, 0, tiled=True)


def _combine_kernel(parts_ref, w_ref, out_ref):
    n, slab, width = parts_ref.shape
    heads = width // HD - 1
    lane = lax.broadcasted_iota(jnp.int32, (slab, HD), 1)
    coded = [parts_ref[i, :, pl.ds(heads * HD, HD)].astype(jnp.float32) for i in range(n)]
    columns = []
    for h in range(heads):
        pick = (lane % 8 == h) & (lane < 24)
        log_weight = [jnp.sum(jnp.where(pick, c, 0.0), axis=1, keepdims=True) for c in coded]
        top = log_weight[0]
        for w in log_weight[1:]:
            top = jnp.maximum(top, w)
        factor = [jnp.exp(w - top) for w in log_weight]
        total = factor[0]
        for f in factor[1:]:
            total = total + f
        numer = jnp.zeros((slab, HD), jnp.float32)
        for i in range(n):
            numer = numer + factor[i] * parts_ref[i, :, pl.ds(h * HD, HD)].astype(jnp.float32)
        columns.append(numer / total)
    attn = jnp.concatenate(columns, axis=1).astype(jnp.bfloat16)
    out_ref[...] = jnp.dot(attn, w_ref[...], preferred_element_type=jnp.float32).astype(out_ref.dtype)


def _combine_project(parts, w_out):
    vmem = pl.BlockSpec(memory_space=pltpu.VMEM)
    return pl.pallas_call(
        _combine_kernel,
        out_shape=jax.ShapeDtypeStruct((parts.shape[1], w_out.shape[1]), jnp.bfloat16),
        in_specs=[vmem] * 2,
        out_specs=vmem,
    )(parts, w_out)


def _split_patch(mesh):
    patch = mesh.devices[:, 0]
    sizes = [len({d.coords[k] for d in patch}) for k in range(3)]
    sizes = [n for n in sizes if n > 1]
    if math.prod(sizes) != patch.shape[0] or len(sizes) < 2:
        return mesh, ("patch",)
    names = tuple(f"patch{k}" for k in range(len(sizes)))
    devices = mesh.devices.reshape(*sizes, mesh.devices.shape[1])
    return jax.sharding.Mesh(devices, names + ("head",)), names


PATCH = ("patch",)


def solution(mesh):
    global PATCH
    mesh, PATCH = _split_patch(mesh)
    placed = (
        P((*PATCH, "head"), None),
        P(),
        P(),
        P(),
        P(None, None, "head"),
        P("head", None),
        P("head"),
        P("head"),
        P(None, PATCH, "head"),
    )
    return jax.shard_map(
        per_device,
        mesh=mesh,
        in_specs=placed,
        out_specs=(P((*PATCH, "head"), None), P(None, PATCH, "head")),
        check_vma=False,
    )
```

```python
import math

import jax
import jax.numpy as jnp
from jax import lax
from jax.experimental import pallas as pl
from jax.experimental.pallas import tpu as pltpu
from jax.sharding import PartitionSpec as P

HD = 128


def modulate(x_tokens, shift, scale_mod):
    values_f = x_tokens.astype(jnp.float32)
    center = jnp.mean(values_f, axis=-1, keepdims=True)
    spread = jnp.mean((values_f - center) * (values_f - center), axis=-1, keepdims=True)
    return ((values_f - center) * lax.rsqrt(spread + 1e-06) * (1.0 + scale_mod) + shift).astype(
        jnp.bfloat16
    )


def per_device(x_tokens, shift, scale_mod, gate, w_qkv, w_out, gain_q, gain_k, stale_kv):
    width = w_qkv.shape[1]
    raw, squares = _modulate_project(
        lax.all_gather(x_tokens, "head", axis=0, tiled=True), shift, scale_mod, w_qkv
    )
    squares = jnp.sum(lax.all_gather(squares, "head"), axis=0).T
    inverse = lax.rsqrt(squares / width + 1e-06)
    queries = (raw[0] * inverse[0][:, None] * gain_q).astype(jnp.bfloat16)
    keys = (raw[1] * inverse[1][:, None] * gain_k).astype(jnp.bfloat16)
    values = raw[2].astype(jnp.bfloat16)
    fresh_kv = jnp.stack([keys, values])
    parts = _exchange_attention(stale_kv, queries, keys, values)
    own_rows = x_tokens.shape[0]
    groups = queries.shape[0] // own_rows
    whole_terms = _combine_project(parts, w_out)
    pieces = lax.all_to_all(
        whole_terms.reshape(groups, own_rows, whole_terms.shape[1]), "head", 0, 0, tiled=True
    )
    projected = jnp.sum(pieces.astype(jnp.float32), axis=0)
    update = (projected * gate).astype(jnp.bfloat16)
    return (update, fresh_kv)


def _modulate_project_kernel(x_ref, shift_ref, scale_ref, w_ref, raw_ref, squares_ref):
    values_f = x_ref[...].astype(jnp.float32)
    center = jnp.mean(values_f, axis=-1, keepdims=True)
    spread = jnp.mean((values_f - center) * (values_f - center), axis=-1, keepdims=True)
    normed = (values_f - center) * lax.rsqrt(spread + 1e-06) * (1.0 + scale_ref[...]) + shift_ref[...]
    normed = normed.astype(jnp.bfloat16)
    lane = lax.broadcasted_iota(jnp.int32, (x_ref.shape[0], HD), 1)
    sums = jnp.zeros((x_ref.shape[0], HD), jnp.float32)
    for c in range(w_ref.shape[0]):
        raw = jnp.dot(normed, w_ref[c], preferred_element_type=jnp.float32)
        raw_ref[c] = raw
        if c < 2:
            sums = jnp.where(lane == c, jnp.sum(raw * raw, axis=1, keepdims=True), sums)
    squares_ref[...] = sums


def _modulate_project(x, shift, scale_mod, w_qkv):
    vmem = pl.BlockSpec(memory_space=pltpu.VMEM)
    rows = x.shape[0]
    raw, sums = pl.pallas_call(
        _modulate_project_kernel,
        out_shape=(
            jax.ShapeDtypeStruct((w_qkv.shape[0], rows, w_qkv.shape[2]), jnp.float32),
            jax.ShapeDtypeStruct((rows, HD), jnp.float32),
        ),
        in_specs=[vmem] * 4,
        out_specs=(vmem, vmem),
        compiler_params=pltpu.CompilerParams(vmem_limit_bytes=48 * 1024 * 1024),
    )(x, shift.reshape(1, -1), scale_mod.reshape(1, -1), w_qkv)
    return raw, sums[:, :2]


def _partial_kernel(mask_ref, q_ref, k_ref, v_ref, kv_ref, out_ref):
    queries_n = q_ref.shape[0]
    slab = k_ref.shape[0]
    count = kv_ref.shape[1] // slab
    heads = q_ref.shape[1] // HD
    scale = math.sqrt(HD)
    is_own = mask_ref[...] > 0
    fresh_col = jnp.max(mask_ref[...], axis=0, keepdims=True) > 0
    contract_minor = (((1,), (1,)), ((), ()))
    contract_major = (((0,), (0,)), ((), ()))
    lane = lax.broadcasted_iota(jnp.int32, (queries_n, HD), 1)
    spread = jnp.zeros((queries_n, HD), jnp.float32)
    for h in range(heads):
        cols = pl.ds(h * HD, HD)
        query = q_ref[:, cols]
        scores = lax.dot_general(
            kv_ref[0, :, cols], query, contract_minor,
            preferred_element_type=jnp.float32,
        ) / scale
        scores = scores.reshape(count, slab, queries_n)
        block_max = jnp.max(scores, axis=1)
        expo = jnp.exp(scores - block_max[:, None, :])
        totals = jnp.sum(expo, axis=1)
        weights = expo.astype(jnp.bfloat16).astype(jnp.float32)
        fresh_scores = lax.dot_general(
            k_ref[:, cols], query, contract_minor, preferred_element_type=jnp.float32
        ) / scale
        fresh_max = jnp.max(fresh_scores, axis=0, keepdims=True)
        fresh_expo = jnp.exp(fresh_scores - fresh_max)
        fresh_total = jnp.sum(fresh_expo, axis=0, keepdims=True)
        fresh_weights = fresh_expo.astype(jnp.bfloat16).astype(jnp.float32)
        top = jnp.max(jnp.where(is_own, -jnp.inf, block_max), axis=0, keepdims=True)
        top = jnp.maximum(top, jnp.where(fresh_col, fresh_max, -jnp.inf))
        factor = jnp.where(is_own, 0.0, jnp.exp(block_max - top))
        fresh_factor = jnp.where(fresh_col, jnp.exp(fresh_max - top), 0.0)
        total = jnp.sum(factor * totals, axis=0, keepdims=True) + fresh_factor * fresh_total
        mixed = (factor[:, None, :] * weights).reshape(count * slab, queries_n)
        numer = lax.dot_general(
            mixed,
            kv_ref[1, :, cols].astype(jnp.float32),
            contract_major,
            preferred_element_type=jnp.float32,
            precision=lax.Precision.HIGHEST,
        )
        numer = numer + lax.dot_general(
            fresh_factor * fresh_weights,
            v_ref[:, cols].astype(jnp.float32),
            contract_major,
            preferred_element_type=jnp.float32,
            precision=lax.Precision.HIGHEST,
        )
        out_ref[:, cols] = (numer / total.reshape(queries_n, 1)).astype(out_ref.dtype)
        log_weight = (top + jnp.log(total)).reshape(queries_n, 1)
        spread = jnp.where(lane % 8 == h, log_weight, spread)
    high = spread.astype(jnp.bfloat16).astype(jnp.float32)
    middle = (spread - high).astype(jnp.bfloat16).astype(jnp.float32)
    low = spread - high - middle
    coded = jnp.where(lane < 8, high, jnp.where(lane < 16, middle, jnp.where(lane < 24, low, 0.0)))
    out_ref[:, pl.ds(heads * HD, HD)] = coded.astype(out_ref.dtype)


def _partial_attention(mask, group_queries, keys, values, near_kv):
    vmem = pl.BlockSpec(memory_space=pltpu.VMEM)
    rows, width = group_queries.shape
    return pl.pallas_call(
        _partial_kernel,
        out_shape=jax.ShapeDtypeStruct((rows, width + HD), jnp.bfloat16),
        in_specs=[vmem] * 5,
        out_specs=vmem,
        compiler_params=pltpu.CompilerParams(vmem_limit_bytes=48 * 1024 * 1024),
    )(mask, group_queries, keys, values, near_kv)


def _exchange_attention(stale_kv, queries, keys, values):
    slab, width = queries.shape
    kv_axes, q_axes = PATCH[-1:], PATCH[:-1]
    m = math.prod(lax.psum(1, name) for name in kv_axes)
    spread_kv = jnp.broadcast_to(stale_kv[:, None], (2, m) + stale_kv.shape[1:])
    near_kv = lax.all_to_all(spread_kv.reshape(2, m * slab, width), kv_axes, 1, 1, tiled=True)
    count = near_kv.shape[1] // slab
    n = math.prod(lax.psum(1, name) for name in q_axes)
    spread = jnp.broadcast_to(queries[None], (n, slab, width)).reshape(n * slab, width)
    group_queries = lax.all_to_all(spread, q_axes, 0, 0, tiled=True)
    block_ids = jnp.arange(count, dtype=jnp.int32)[:, None]
    slab_ids = (jnp.arange(n * slab, dtype=jnp.int32) // slab)[None, :]
    mask = (block_ids == lax.axis_index(kv_axes)) & (slab_ids == lax.axis_index(q_axes))
    partial = _partial_attention(mask.astype(jnp.int32), group_queries, keys, values, near_kv)
    return lax.all_to_all(partial.reshape(n, slab, width + HD), q_axes, 0, 0, tiled=True)


def _combine_kernel(parts_ref, w_ref, out_ref):
    n, slab, width = parts_ref.shape
    heads = width // HD - 1
    lane = lax.broadcasted_iota(jnp.int32, (slab, HD), 1)
    coded = [parts_ref[i, :, pl.ds(heads * HD, HD)].astype(jnp.float32) for i in range(n)]
    columns = []
    for h in range(heads):
        pick = (lane % 8 == h) & (lane < 24)
        log_weight = [jnp.sum(jnp.where(pick, c, 0.0), axis=1, keepdims=True) for c in coded]
        top = log_weight[0]
        for w in log_weight[1:]:
            top = jnp.maximum(top, w)
        factor = [jnp.exp(w - top) for w in log_weight]
        total = factor[0]
        for f in factor[1:]:
            total = total + f
        numer = jnp.zeros((slab, HD), jnp.float32)
        for i in range(n):
            numer = numer + factor[i] * parts_ref[i, :, pl.ds(h * HD, HD)].astype(jnp.float32)
        columns.append(numer / total)
    attn = jnp.concatenate(columns, axis=1).astype(jnp.bfloat16)
    out_ref[...] = jnp.dot(attn, w_ref[...], preferred_element_type=jnp.float32).astype(out_ref.dtype)


def _combine_project(parts, w_out):
    vmem = pl.BlockSpec(memory_space=pltpu.VMEM)
    return pl.pallas_call(
        _combine_kernel,
        out_shape=jax.ShapeDtypeStruct((parts.shape[1], w_out.shape[1]), jnp.bfloat16),
        in_specs=[vmem] * 2,
        out_specs=vmem,
    )(parts, w_out)


def _split_patch(mesh):
    patch = mesh.devices[:, 0]
    sizes = [len({d.coords[k] for d in patch}) for k in range(3)]
    sizes = [n for n in sizes if n > 1]
    if math.prod(sizes) != patch.shape[0] or len(sizes) < 2:
        return mesh, ("patch",)
    names = tuple(f"patch{k}" for k in range(len(sizes)))
    devices = mesh.devices.reshape(*sizes, mesh.devices.shape[1])
    return jax.sharding.Mesh(devices, names + ("head",)), names


PATCH = ("patch",)


def solution(mesh):
    global PATCH
    mesh, PATCH = _split_patch(mesh)
    placed = (
        P((*PATCH, "head"), None),
        P(),
        P(),
        P(),
        P(None, None, "head"),
        P("head", None),
        P("head"),
        P("head"),
        P(None, PATCH, "head"),
    )
    return jax.shard_map(
        per_device,
        mesh=mesh,
        in_specs=placed,
        out_specs=(P((*PATCH, "head"), None), P(None, PATCH, "head")),
        check_vma=False,
    )
```

```python
import math

import jax
import jax.numpy as jnp
from jax import lax
from jax.experimental import pallas as pl
from jax.experimental.pallas import tpu as pltpu
from jax.sharding import PartitionSpec as P

HD = 128


def modulate(x_tokens, shift, scale_mod):
    values_f = x_tokens.astype(jnp.float32)
    center = jnp.mean(values_f, axis=-1, keepdims=True)
    spread = jnp.mean((values_f - center) * (values_f - center), axis=-1, keepdims=True)
    return ((values_f - center) * lax.rsqrt(spread + 1e-06) * (1.0 + scale_mod) + shift).astype(
        jnp.bfloat16
    )


def per_device(x_tokens, shift, scale_mod, gate, w_qkv, w_out, gain_q, gain_k, stale_kv):
    width = w_qkv.shape[1]
    raw, squares = _modulate_project(
        lax.all_gather(x_tokens, "head", axis=0, tiled=True), shift, scale_mod, w_qkv
    )
    squares = jnp.sum(lax.all_gather(squares, "head"), axis=0).T
    inverse = lax.rsqrt(squares / width + 1e-06)
    queries = (raw[0] * inverse[0][:, None] * gain_q).astype(jnp.bfloat16)
    keys = (raw[1] * inverse[1][:, None] * gain_k).astype(jnp.bfloat16)
    values = raw[2].astype(jnp.bfloat16)
    fresh_kv = jnp.stack([keys, values])
    parts = _exchange_attention(stale_kv, queries, keys, values)
    own_rows = x_tokens.shape[0]
    groups = queries.shape[0] // own_rows
    whole_terms = _combine_project(parts, w_out)
    pieces = lax.all_to_all(
        whole_terms.reshape(groups, own_rows, whole_terms.shape[1]), "head", 0, 0, tiled=True
    )
    projected = jnp.sum(pieces.astype(jnp.float32), axis=0)
    update = (projected * gate).astype(jnp.bfloat16)
    return (update, fresh_kv)


def _modulate_project_kernel(x_ref, shift_ref, scale_ref, w_ref, raw_ref, squares_ref):
    values_f = x_ref[...].astype(jnp.float32)
    center = jnp.mean(values_f, axis=-1, keepdims=True)
    spread = jnp.mean((values_f - center) * (values_f - center), axis=-1, keepdims=True)
    scale = scale_ref[...].reshape(1, -1)
    shift = shift_ref[...].reshape(1, -1)
    normed = (values_f - center) * lax.rsqrt(spread + 1e-06) * (1.0 + scale) + shift
    normed = normed.astype(jnp.bfloat16)
    lane = lax.broadcasted_iota(jnp.int32, (x_ref.shape[0], HD), 1)
    sums = jnp.zeros((x_ref.shape[0], HD), jnp.float32)
    for c in range(w_ref.shape[0]):
        raw = jnp.dot(normed, w_ref[c], preferred_element_type=jnp.float32)
        raw_ref[c] = raw
        if c < 2:
            sums = jnp.where(lane == c, jnp.sum(raw * raw, axis=1, keepdims=True), sums)
    squares_ref[...] = sums


def _modulate_project(x, shift, scale_mod, w_qkv):
    vmem = pl.BlockSpec(memory_space=pltpu.VMEM)
    rows = x.shape[0]
    raw, sums = pl.pallas_call(
        _modulate_project_kernel,
        out_shape=(
            jax.ShapeDtypeStruct((w_qkv.shape[0], rows, w_qkv.shape[2]), jnp.float32),
            jax.ShapeDtypeStruct((rows, HD), jnp.float32),
        ),
        in_specs=[vmem] * 4,
        out_specs=(vmem, vmem),
        compiler_params=pltpu.CompilerParams(vmem_limit_bytes=48 * 1024 * 1024),
    )(x, shift, scale_mod, w_qkv)
    return raw, sums[:, :2]


def _partial_kernel(mask_ref, q_ref, k_ref, v_ref, kv_ref, out_ref):
    queries_n = q_ref.shape[0]
    slab = k_ref.shape[0]
    count = kv_ref.shape[1] // slab
    heads = q_ref.shape[1] // HD
    scale = math.sqrt(HD)
    is_own = mask_ref[...] > 0
    fresh_col = jnp.max(mask_ref[...], axis=0, keepdims=True) > 0
    contract_minor = (((1,), (1,)), ((), ()))
    contract_major = (((0,), (0,)), ((), ()))
    lane = lax.broadcasted_iota(jnp.int32, (queries_n, HD), 1)
    spread = jnp.zeros((queries_n, HD), jnp.float32)
    for h in range(heads):
        cols = pl.ds(h * HD, HD)
        query = q_ref[:, cols]
        scores = lax.dot_general(
            kv_ref[0, :, cols], query, contract_minor,
            preferred_element_type=jnp.float32,
        ) / scale
        scores = scores.reshape(count, slab, queries_n)
        block_max = jnp.max(scores, axis=1)
        expo = jnp.exp(scores - block_max[:, None, :])
        totals = jnp.sum(expo, axis=1)
        weights = expo.astype(jnp.bfloat16).astype(jnp.float32)
        fresh_scores = lax.dot_general(
            k_ref[:, cols], query, contract_minor, preferred_element_type=jnp.float32
        ) / scale
        fresh_max = jnp.max(fresh_scores, axis=0, keepdims=True)
        fresh_expo = jnp.exp(fresh_scores - fresh_max)
        fresh_total = jnp.sum(fresh_expo, axis=0, keepdims=True)
        fresh_weights = fresh_expo.astype(jnp.bfloat16).astype(jnp.float32)
        top = jnp.max(jnp.where(is_own, -jnp.inf, block_max), axis=0, keepdims=True)
        top = jnp.maximum(top, jnp.where(fresh_col, fresh_max, -jnp.inf))
        factor = jnp.where(is_own, 0.0, jnp.exp(block_max - top))
        fresh_factor = jnp.where(fresh_col, jnp.exp(fresh_max - top), 0.0)
        total = jnp.sum(factor * totals, axis=0, keepdims=True) + fresh_factor * fresh_total
        mixed = (factor[:, None, :] * weights).reshape(count * slab, queries_n)
        numer = lax.dot_general(
            mixed,
            kv_ref[1, :, cols].astype(jnp.float32),
            contract_major,
            preferred_element_type=jnp.float32,
            precision=lax.Precision.HIGHEST,
        )
        numer = numer + lax.dot_general(
            fresh_factor * fresh_weights,
            v_ref[:, cols].astype(jnp.float32),
            contract_major,
            preferred_element_type=jnp.float32,
            precision=lax.Precision.HIGHEST,
        )
        out_ref[:, cols] = (numer / total.reshape(queries_n, 1)).astype(out_ref.dtype)
        log_weight = (top + jnp.log(total)).reshape(queries_n, 1)
        spread = jnp.where(lane % 8 == h, log_weight, spread)
    high = spread.astype(jnp.bfloat16).astype(jnp.float32)
    middle = (spread - high).astype(jnp.bfloat16).astype(jnp.float32)
    low = spread - high - middle
    coded = jnp.where(lane < 8, high, jnp.where(lane < 16, middle, jnp.where(lane < 24, low, 0.0)))
    out_ref[:, pl.ds(heads * HD, HD)] = coded.astype(out_ref.dtype)


def _partial_attention(mask, group_queries, keys, values, near_kv):
    vmem = pl.BlockSpec(memory_space=pltpu.VMEM)
    rows, width = group_queries.shape
    return pl.pallas_call(
        _partial_kernel,
        out_shape=jax.ShapeDtypeStruct((rows, width + HD), jnp.bfloat16),
        in_specs=[vmem] * 5,
        out_specs=vmem,
        compiler_params=pltpu.CompilerParams(vmem_limit_bytes=48 * 1024 * 1024),
    )(mask, group_queries, keys, values, near_kv)


def _exchange_attention(stale_kv, queries, keys, values):
    slab, width = queries.shape
    kv_axes, q_axes = PATCH[-1:], PATCH[:-1]
    m = math.prod(lax.psum(1, name) for name in kv_axes)
    spread_kv = jnp.broadcast_to(stale_kv[:, None], (2, m) + stale_kv.shape[1:])
    near_kv = lax.all_to_all(spread_kv.reshape(2, m * slab, width), kv_axes, 1, 1, tiled=True)
    count = near_kv.shape[1] // slab
    n = math.prod(lax.psum(1, name) for name in q_axes)
    spread = jnp.broadcast_to(queries[None], (n, slab, width)).reshape(n * slab, width)
    group_queries = lax.all_to_all(spread, q_axes, 0, 0, tiled=True)
    block_ids = jnp.arange(count, dtype=jnp.int32)[:, None]
    slab_ids = (jnp.arange(n * slab, dtype=jnp.int32) // slab)[None, :]
    mask = (block_ids == lax.axis_index(kv_axes)) & (slab_ids == lax.axis_index(q_axes))
    partial = _partial_attention(mask.astype(jnp.int32), group_queries, keys, values, near_kv)
    return lax.all_to_all(partial.reshape(n, slab, width + HD), q_axes, 0, 0, tiled=True)


def _combine_kernel(parts_ref, w_ref, out_ref):
    n, slab, width = parts_ref.shape
    heads = width // HD - 1
    lane = lax.broadcasted_iota(jnp.int32, (slab, HD), 1)
    coded = [parts_ref[i, :, pl.ds(heads * HD, HD)].astype(jnp.float32) for i in range(n)]
    columns = []
    for h in range(heads):
        pick = (lane % 8 == h) & (lane < 24)
        log_weight = [jnp.sum(jnp.where(pick, c, 0.0), axis=1, keepdims=True) for c in coded]
        top = log_weight[0]
        for w in log_weight[1:]:
            top = jnp.maximum(top, w)
        factor = [jnp.exp(w - top) for w in log_weight]
        total = factor[0]
        for f in factor[1:]:
            total = total + f
        numer = jnp.zeros((slab, HD), jnp.float32)
        for i in range(n):
            numer = numer + factor[i] * parts_ref[i, :, pl.ds(h * HD, HD)].astype(jnp.float32)
        columns.append(numer / total)
    attn = jnp.concatenate(columns, axis=1).astype(jnp.bfloat16)
    out_ref[...] = jnp.dot(attn, w_ref[...], preferred_element_type=jnp.float32).astype(out_ref.dtype)


def _combine_project(parts, w_out):
    vmem = pl.BlockSpec(memory_space=pltpu.VMEM)
    return pl.pallas_call(
        _combine_kernel,
        out_shape=jax.ShapeDtypeStruct((parts.shape[1], w_out.shape[1]), jnp.bfloat16),
        in_specs=[vmem] * 2,
        out_specs=vmem,
    )(parts, w_out)


def _split_patch(mesh):
    patch = mesh.devices[:, 0]
    sizes = [len({d.coords[k] for d in patch}) for k in range(3)]
    sizes = [n for n in sizes if n > 1]
    if math.prod(sizes) != patch.shape[0] or len(sizes) < 2:
        return mesh, ("patch",)
    names = tuple(f"patch{k}" for k in range(len(sizes)))
    devices = mesh.devices.reshape(*sizes, mesh.devices.shape[1])
    return jax.sharding.Mesh(devices, names + ("head",)), names


PATCH = ("patch",)


def solution(mesh):
    global PATCH
    mesh, PATCH = _split_patch(mesh)
    placed = (
        P((*PATCH, "head"), None),
        P(),
        P(),
        P(),
        P(None, None, "head"),
        P("head", None),
        P("head"),
        P("head"),
        P(None, PATCH, "head"),
    )
    return jax.shard_map(
        per_device,
        mesh=mesh,
        in_specs=placed,
        out_specs=(P((*PATCH, "head"), None), P(None, PATCH, "head")),
        check_vma=False,
    )
```

```python
import math

import jax
import jax.numpy as jnp
from jax import lax
from jax.experimental import pallas as pl
from jax.experimental.pallas import tpu as pltpu
from jax.sharding import PartitionSpec as P

HD = 128


def modulate(x_tokens, shift, scale_mod):
    values_f = x_tokens.astype(jnp.float32)
    center = jnp.mean(values_f, axis=-1, keepdims=True)
    spread = jnp.mean((values_f - center) * (values_f - center), axis=-1, keepdims=True)
    return ((values_f - center) * lax.rsqrt(spread + 1e-06) * (1.0 + scale_mod) + shift).astype(
        jnp.bfloat16
    )


def per_device(x_tokens, shift, scale_mod, gate, w_qkv, w_out, gain_q, gain_k, stale_kv):
    width = w_qkv.shape[1]
    raw, squares = _modulate_project(
        lax.all_gather(x_tokens, "head", axis=0, tiled=True), shift, scale_mod, w_qkv
    )
    squares = jnp.sum(lax.all_gather(squares, "head"), axis=0).T
    inverse = lax.rsqrt(squares / width + 1e-06)
    queries = (raw[0] * inverse[0][:, None] * gain_q).astype(jnp.bfloat16)
    keys = (raw[1] * inverse[1][:, None] * gain_k).astype(jnp.bfloat16)
    values = raw[2].astype(jnp.bfloat16)
    fresh_kv = jnp.stack([keys, values])
    parts = _exchange_attention(stale_kv, queries, keys, values)
    own_rows = x_tokens.shape[0]
    groups = queries.shape[0] // own_rows
    whole_terms = _combine_project(parts, w_out)
    pieces = lax.all_to_all(
        whole_terms.reshape(groups, own_rows, whole_terms.shape[1]), "head", 0, 0, tiled=True
    )
    projected = jnp.sum(pieces.astype(jnp.float32), axis=0)
    update = (projected * gate).astype(jnp.bfloat16)
    return (update, fresh_kv)


def _modulate_project_kernel(x_ref, mod_ref, w_ref, raw_ref, squares_ref):
    c = pl.program_id(0)
    values_f = x_ref[...].astype(jnp.float32)
    center = jnp.mean(values_f, axis=-1, keepdims=True)
    spread = jnp.mean((values_f - center) * (values_f - center), axis=-1, keepdims=True)
    shift = mod_ref[pl.ds(0, 1), :]
    scale = mod_ref[pl.ds(1, 1), :]
    normed = (values_f - center) * lax.rsqrt(spread + 1e-06) * (1.0 + scale) + shift
    raw = jnp.dot(normed.astype(jnp.bfloat16), w_ref[0], preferred_element_type=jnp.float32)
    raw_ref[0] = raw

    @pl.when(c == 0)
    def _():
        squares_ref[...] = jnp.zeros(squares_ref.shape, jnp.float32)

    lane = lax.broadcasted_iota(jnp.int32, squares_ref.shape, 1)
    sums = jnp.sum(raw * raw, axis=1, keepdims=True)
    squares_ref[...] = jnp.where((lane == c) & (c < 2), sums, squares_ref[...])


def _modulate_project(x, shift, scale_mod, w_qkv):
    rows, width = x.shape
    parts, _, cols = w_qkv.shape
    raw, sums = pl.pallas_call(
        _modulate_project_kernel,
        out_shape=(
            jax.ShapeDtypeStruct((parts, rows, cols), jnp.float32),
            jax.ShapeDtypeStruct((rows, HD), jnp.float32),
        ),
        grid=(parts,),
        in_specs=[
            pl.BlockSpec((rows, width), lambda c: (0, 0)),
            pl.BlockSpec((2, width), lambda c: (0, 0)),
            pl.BlockSpec((1, width, cols), lambda c: (c, 0, 0)),
        ],
        out_specs=(
            pl.BlockSpec((1, rows, cols), lambda c: (c, 0, 0)),
            pl.BlockSpec((rows, HD), lambda c: (0, 0)),
        ),
    )(x, jnp.stack([shift, scale_mod]), w_qkv)
    return raw, sums[:, :2]


def _partial_kernel(mask_ref, q_ref, k_ref, v_ref, kv_ref, out_ref):
    queries_n = q_ref.shape[0]
    slab = k_ref.shape[0]
    count = kv_ref.shape[1] // slab
    heads = q_ref.shape[1] // HD
    scale = math.sqrt(HD)
    is_own = mask_ref[...] > 0
    fresh_col = jnp.max(mask_ref[...], axis=0, keepdims=True) > 0
    contract_minor = (((1,), (1,)), ((), ()))
    contract_major = (((0,), (0,)), ((), ()))
    lane = lax.broadcasted_iota(jnp.int32, (queries_n, HD), 1)
    spread = jnp.zeros((queries_n, HD), jnp.float32)
    for h in range(heads):
        cols = pl.ds(h * HD, HD)
        query = q_ref[:, cols]
        scores = lax.dot_general(
            kv_ref[0, :, cols], query, contract_minor,
            preferred_element_type=jnp.float32,
        ) / scale
        scores = scores.reshape(count, slab, queries_n)
        block_max = jnp.max(scores, axis=1)
        expo = jnp.exp(scores - block_max[:, None, :])
        totals = jnp.sum(expo, axis=1)
        weights = expo.astype(jnp.bfloat16).astype(jnp.float32)
        fresh_scores = lax.dot_general(
            k_ref[:, cols], query, contract_minor, preferred_element_type=jnp.float32
        ) / scale
        fresh_max = jnp.max(fresh_scores, axis=0, keepdims=True)
        fresh_expo = jnp.exp(fresh_scores - fresh_max)
        fresh_total = jnp.sum(fresh_expo, axis=0, keepdims=True)
        fresh_weights = fresh_expo.astype(jnp.bfloat16).astype(jnp.float32)
        top = jnp.max(jnp.where(is_own, -jnp.inf, block_max), axis=0, keepdims=True)
        top = jnp.maximum(top, jnp.where(fresh_col, fresh_max, -jnp.inf))
        factor = jnp.where(is_own, 0.0, jnp.exp(block_max - top))
        fresh_factor = jnp.where(fresh_col, jnp.exp(fresh_max - top), 0.0)
        total = jnp.sum(factor * totals, axis=0, keepdims=True) + fresh_factor * fresh_total
        mixed = (factor[:, None, :] * weights).reshape(count * slab, queries_n)
        numer = lax.dot_general(
            mixed,
            kv_ref[1, :, cols].astype(jnp.float32),
            contract_major,
            preferred_element_type=jnp.float32,
            precision=lax.Precision.HIGHEST,
        )
        numer = numer + lax.dot_general(
            fresh_factor * fresh_weights,
            v_ref[:, cols].astype(jnp.float32),
            contract_major,
            preferred_element_type=jnp.float32,
            precision=lax.Precision.HIGHEST,
        )
        out_ref[:, cols] = (numer / total.reshape(queries_n, 1)).astype(out_ref.dtype)
        log_weight = (top + jnp.log(total)).reshape(queries_n, 1)
        spread = jnp.where(lane % 8 == h, log_weight, spread)
    high = spread.astype(jnp.bfloat16).astype(jnp.float32)
    middle = (spread - high).astype(jnp.bfloat16).astype(jnp.float32)
    low = spread - high - middle
    coded = jnp.where(lane < 8, high, jnp.where(lane < 16, middle, jnp.where(lane < 24, low, 0.0)))
    out_ref[:, pl.ds(heads * HD, HD)] = coded.astype(out_ref.dtype)


def _partial_attention(mask, group_queries, keys, values, near_kv):
    vmem = pl.BlockSpec(memory_space=pltpu.VMEM)
    rows, width = group_queries.shape
    return pl.pallas_call(
        _partial_kernel,
        out_shape=jax.ShapeDtypeStruct((rows, width + HD), jnp.bfloat16),
        in_specs=[vmem] * 5,
        out_specs=vmem,
        compiler_params=pltpu.CompilerParams(vmem_limit_bytes=48 * 1024 * 1024),
    )(mask, group_queries, keys, values, near_kv)


def _exchange_attention(stale_kv, queries, keys, values):
    slab, width = queries.shape
    kv_axes, q_axes = PATCH[-1:], PATCH[:-1]
    m = math.prod(lax.psum(1, name) for name in kv_axes)
    spread_kv = jnp.broadcast_to(stale_kv[:, None], (2, m) + stale_kv.shape[1:])
    near_kv = lax.all_to_all(spread_kv.reshape(2, m * slab, width), kv_axes, 1, 1, tiled=True)
    count = near_kv.shape[1] // slab
    n = math.prod(lax.psum(1, name) for name in q_axes)
    spread = jnp.broadcast_to(queries[None], (n, slab, width)).reshape(n * slab, width)
    group_queries = lax.all_to_all(spread, q_axes, 0, 0, tiled=True)
    block_ids = jnp.arange(count, dtype=jnp.int32)[:, None]
    slab_ids = (jnp.arange(n * slab, dtype=jnp.int32) // slab)[None, :]
    mask = (block_ids == lax.axis_index(kv_axes)) & (slab_ids == lax.axis_index(q_axes))
    partial = _partial_attention(mask.astype(jnp.int32), group_queries, keys, values, near_kv)
    return lax.all_to_all(partial.reshape(n, slab, width + HD), q_axes, 0, 0, tiled=True)


def _combine_kernel(parts_ref, w_ref, out_ref):
    n, slab, width = parts_ref.shape
    heads = width // HD - 1
    lane = lax.broadcasted_iota(jnp.int32, (slab, HD), 1)
    coded = [parts_ref[i, :, pl.ds(heads * HD, HD)].astype(jnp.float32) for i in range(n)]
    columns = []
    for h in range(heads):
        pick = (lane % 8 == h) & (lane < 24)
        log_weight = [jnp.sum(jnp.where(pick, c, 0.0), axis=1, keepdims=True) for c in coded]
        top = log_weight[0]
        for w in log_weight[1:]:
            top = jnp.maximum(top, w)
        factor = [jnp.exp(w - top) for w in log_weight]
        total = factor[0]
        for f in factor[1:]:
            total = total + f
        numer = jnp.zeros((slab, HD), jnp.float32)
        for i in range(n):
            numer = numer + factor[i] * parts_ref[i, :, pl.ds(h * HD, HD)].astype(jnp.float32)
        columns.append(numer / total)
    attn = jnp.concatenate(columns, axis=1).astype(jnp.bfloat16)
    out_ref[...] = jnp.dot(attn, w_ref[...], preferred_element_type=jnp.float32).astype(out_ref.dtype)


def _combine_project(parts, w_out):
    vmem = pl.BlockSpec(memory_space=pltpu.VMEM)
    return pl.pallas_call(
        _combine_kernel,
        out_shape=jax.ShapeDtypeStruct((parts.shape[1], w_out.shape[1]), jnp.bfloat16),
        in_specs=[vmem] * 2,
        out_specs=vmem,
    )(parts, w_out)


def _split_patch(mesh):
    patch = mesh.devices[:, 0]
    sizes = [len({d.coords[k] for d in patch}) for k in range(3)]
    sizes = [n for n in sizes if n > 1]
    if math.prod(sizes) != patch.shape[0] or len(sizes) < 2:
        return mesh, ("patch",)
    names = tuple(f"patch{k}" for k in range(len(sizes)))
    devices = mesh.devices.reshape(*sizes, mesh.devices.shape[1])
    return jax.sharding.Mesh(devices, names + ("head",)), names


PATCH = ("patch",)


def solution(mesh):
    global PATCH
    mesh, PATCH = _split_patch(mesh)
    placed = (
        P((*PATCH, "head"), None),
        P(),
        P(),
        P(),
        P(None, None, "head"),
        P("head", None),
        P("head"),
        P("head"),
        P(None, PATCH, "head"),
    )
    return jax.shard_map(
        per_device,
        mesh=mesh,
        in_specs=placed,
        out_specs=(P((*PATCH, "head"), None), P(None, PATCH, "head")),
        check_vma=False,
    )
```

```python
import math

import jax
import jax.numpy as jnp
from jax import lax
from jax.experimental import pallas as pl
from jax.experimental.pallas import tpu as pltpu
from jax.sharding import PartitionSpec as P

HD = 128


def modulate(x_tokens, shift, scale_mod):
    values_f = x_tokens.astype(jnp.float32)
    center = jnp.mean(values_f, axis=-1, keepdims=True)
    spread = jnp.mean((values_f - center) * (values_f - center), axis=-1, keepdims=True)
    return ((values_f - center) * lax.rsqrt(spread + 1e-06) * (1.0 + scale_mod) + shift).astype(
        jnp.bfloat16
    )


def per_device(x_tokens, shift, scale_mod, gate, w_qkv, w_out, gain_q, gain_k, stale_kv):
    width = w_qkv.shape[1]
    raw, squares = _modulate_project(
        lax.all_gather(x_tokens, "head", axis=0, tiled=True), shift, scale_mod, w_qkv
    )
    squares = jnp.sum(lax.all_gather(squares, "head"), axis=0).T
    inverse = lax.rsqrt(squares / width + 1e-06)
    queries = (raw[0] * inverse[0][:, None] * gain_q).astype(jnp.bfloat16)
    keys = (raw[1] * inverse[1][:, None] * gain_k).astype(jnp.bfloat16)
    values = raw[2].astype(jnp.bfloat16)
    fresh_kv = jnp.stack([keys, values])
    queries, fresh_kv = lax.optimization_barrier((queries, fresh_kv))
    parts = _exchange_attention(stale_kv, queries, keys, values)
    own_rows = x_tokens.shape[0]
    groups = queries.shape[0] // own_rows
    whole_terms = _combine_project(parts, w_out)
    pieces = lax.all_to_all(
        whole_terms.reshape(groups, own_rows, whole_terms.shape[1]), "head", 0, 0, tiled=True
    )
    projected = jnp.sum(pieces.astype(jnp.float32), axis=0)
    update = (projected * gate).astype(jnp.bfloat16)
    return (update, fresh_kv)


def _modulate_project_kernel(x_ref, shift_ref, scale_ref, w_ref, raw_ref, squares_ref):
    values_f = x_ref[...].astype(jnp.float32)
    center = jnp.mean(values_f, axis=-1, keepdims=True)
    spread = jnp.mean((values_f - center) * (values_f - center), axis=-1, keepdims=True)
    normed = (values_f - center) * lax.rsqrt(spread + 1e-06) * (1.0 + scale_ref[...]) + shift_ref[...]
    normed = normed.astype(jnp.bfloat16)
    lane = lax.broadcasted_iota(jnp.int32, (x_ref.shape[0], HD), 1)
    sums = jnp.zeros((x_ref.shape[0], HD), jnp.float32)
    for c in range(w_ref.shape[0]):
        raw = jnp.dot(normed, w_ref[c], preferred_element_type=jnp.float32)
        raw_ref[c] = raw
        if c < 2:
            sums = jnp.where(lane == c, jnp.sum(raw * raw, axis=1, keepdims=True), sums)
    squares_ref[...] = sums


def _modulate_project(x, shift, scale_mod, w_qkv):
    vmem = pl.BlockSpec(memory_space=pltpu.VMEM)
    rows = x.shape[0]
    raw, sums = pl.pallas_call(
        _modulate_project_kernel,
        out_shape=(
            jax.ShapeDtypeStruct((w_qkv.shape[0], rows, w_qkv.shape[2]), jnp.float32),
            jax.ShapeDtypeStruct((rows, HD), jnp.float32),
        ),
        in_specs=[vmem] * 4,
        out_specs=(vmem, vmem),
        compiler_params=pltpu.CompilerParams(vmem_limit_bytes=48 * 1024 * 1024),
    )(x, shift.reshape(1, -1), scale_mod.reshape(1, -1), w_qkv)
    return raw, sums[:, :2]


def _partial_kernel(mask_ref, q_ref, k_ref, v_ref, kv_ref, out_ref):
    queries_n = q_ref.shape[0]
    slab = k_ref.shape[0]
    count = kv_ref.shape[1] // slab
    heads = q_ref.shape[1] // HD
    scale = math.sqrt(HD)
    is_own = mask_ref[...] > 0
    fresh_col = jnp.max(mask_ref[...], axis=0, keepdims=True) > 0
    contract_minor = (((1,), (1,)), ((), ()))
    contract_major = (((0,), (0,)), ((), ()))
    lane = lax.broadcasted_iota(jnp.int32, (queries_n, HD), 1)
    spread = jnp.zeros((queries_n, HD), jnp.float32)
    for h in range(heads):
        cols = pl.ds(h * HD, HD)
        query = q_ref[:, cols]
        scores = lax.dot_general(
            kv_ref[0, :, cols], query, contract_minor,
            preferred_element_type=jnp.float32,
        ) / scale
        scores = scores.reshape(count, slab, queries_n)
        block_max = jnp.max(scores, axis=1)
        expo = jnp.exp(scores - block_max[:, None, :])
        totals = jnp.sum(expo, axis=1)
        weights = expo.astype(jnp.bfloat16).astype(jnp.float32)
        fresh_scores = lax.dot_general(
            k_ref[:, cols], query, contract_minor, preferred_element_type=jnp.float32
        ) / scale
        fresh_max = jnp.max(fresh_scores, axis=0, keepdims=True)
        fresh_expo = jnp.exp(fresh_scores - fresh_max)
        fresh_total = jnp.sum(fresh_expo, axis=0, keepdims=True)
        fresh_weights = fresh_expo.astype(jnp.bfloat16).astype(jnp.float32)
        top = jnp.max(jnp.where(is_own, -jnp.inf, block_max), axis=0, keepdims=True)
        top = jnp.maximum(top, jnp.where(fresh_col, fresh_max, -jnp.inf))
        factor = jnp.where(is_own, 0.0, jnp.exp(block_max - top))
        fresh_factor = jnp.where(fresh_col, jnp.exp(fresh_max - top), 0.0)
        total = jnp.sum(factor * totals, axis=0, keepdims=True) + fresh_factor * fresh_total
        mixed = (factor[:, None, :] * weights).reshape(count * slab, queries_n)
        numer = lax.dot_general(
            mixed,
            kv_ref[1, :, cols].astype(jnp.float32),
            contract_major,
            preferred_element_type=jnp.float32,
            precision=lax.Precision.HIGHEST,
        )
        numer = numer + lax.dot_general(
            fresh_factor * fresh_weights,
            v_ref[:, cols].astype(jnp.float32),
            contract_major,
            preferred_element_type=jnp.float32,
            precision=lax.Precision.HIGHEST,
        )
        out_ref[:, cols] = (numer / total.reshape(queries_n, 1)).astype(out_ref.dtype)
        log_weight = (top + jnp.log(total)).reshape(queries_n, 1)
        spread = jnp.where(lane % 8 == h, log_weight, spread)
    high = spread.astype(jnp.bfloat16).astype(jnp.float32)
    middle = (spread - high).astype(jnp.bfloat16).astype(jnp.float32)
    low = spread - high - middle
    coded = jnp.where(lane < 8, high, jnp.where(lane < 16, middle, jnp.where(lane < 24, low, 0.0)))
    out_ref[:, pl.ds(heads * HD, HD)] = coded.astype(out_ref.dtype)


def _partial_attention(mask, group_queries, keys, values, near_kv):
    vmem = pl.BlockSpec(memory_space=pltpu.VMEM)
    rows, width = group_queries.shape
    return pl.pallas_call(
        _partial_kernel,
        out_shape=jax.ShapeDtypeStruct((rows, width + HD), jnp.bfloat16),
        in_specs=[vmem] * 5,
        out_specs=vmem,
        compiler_params=pltpu.CompilerParams(vmem_limit_bytes=48 * 1024 * 1024),
    )(mask, group_queries, keys, values, near_kv)


def _exchange_attention(stale_kv, queries, keys, values):
    slab, width = queries.shape
    kv_axes, q_axes = PATCH[-1:], PATCH[:-1]
    m = math.prod(lax.psum(1, name) for name in kv_axes)
    spread_kv = jnp.broadcast_to(stale_kv[:, None], (2, m) + stale_kv.shape[1:])
    near_kv = lax.all_to_all(spread_kv.reshape(2, m * slab, width), kv_axes, 1, 1, tiled=True)
    count = near_kv.shape[1] // slab
    n = math.prod(lax.psum(1, name) for name in q_axes)
    spread = jnp.broadcast_to(queries[None], (n, slab, width)).reshape(n * slab, width)
    group_queries = lax.all_to_all(spread, q_axes, 0, 0, tiled=True)
    block_ids = jnp.arange(count, dtype=jnp.int32)[:, None]
    slab_ids = (jnp.arange(n * slab, dtype=jnp.int32) // slab)[None, :]
    mask = (block_ids == lax.axis_index(kv_axes)) & (slab_ids == lax.axis_index(q_axes))
    partial = _partial_attention(mask.astype(jnp.int32), group_queries, keys, values, near_kv)
    return lax.all_to_all(partial.reshape(n, slab, width + HD), q_axes, 0, 0, tiled=True)


def _combine_kernel(parts_ref, w_ref, out_ref):
    n, slab, width = parts_ref.shape
    heads = width // HD - 1
    lane = lax.broadcasted_iota(jnp.int32, (slab, HD), 1)
    coded = [parts_ref[i, :, pl.ds(heads * HD, HD)].astype(jnp.float32) for i in range(n)]
    columns = []
    for h in range(heads):
        pick = (lane % 8 == h) & (lane < 24)
        log_weight = [jnp.sum(jnp.where(pick, c, 0.0), axis=1, keepdims=True) for c in coded]
        top = log_weight[0]
        for w in log_weight[1:]:
            top = jnp.maximum(top, w)
        factor = [jnp.exp(w - top) for w in log_weight]
        total = factor[0]
        for f in factor[1:]:
            total = total + f
        numer = jnp.zeros((slab, HD), jnp.float32)
        for i in range(n):
            numer = numer + factor[i] * parts_ref[i, :, pl.ds(h * HD, HD)].astype(jnp.float32)
        columns.append(numer / total)
    attn = jnp.concatenate(columns, axis=1).astype(jnp.bfloat16)
    out_ref[...] = jnp.dot(attn, w_ref[...], preferred_element_type=jnp.float32).astype(out_ref.dtype)


def _combine_project(parts, w_out):
    vmem = pl.BlockSpec(memory_space=pltpu.VMEM)
    return pl.pallas_call(
        _combine_kernel,
        out_shape=jax.ShapeDtypeStruct((parts.shape[1], w_out.shape[1]), jnp.bfloat16),
        in_specs=[vmem] * 2,
        out_specs=vmem,
    )(parts, w_out)


def _split_patch(mesh):
    patch = mesh.devices[:, 0]
    sizes = [len({d.coords[k] for d in patch}) for k in range(3)]
    sizes = [n for n in sizes if n > 1]
    if math.prod(sizes) != patch.shape[0] or len(sizes) < 2:
        return mesh, ("patch",)
    names = tuple(f"patch{k}" for k in range(len(sizes)))
    devices = mesh.devices.reshape(*sizes, mesh.devices.shape[1])
    return jax.sharding.Mesh(devices, names + ("head",)), names


PATCH = ("patch",)


def solution(mesh):
    global PATCH
    mesh, PATCH = _split_patch(mesh)
    placed = (
        P((*PATCH, "head"), None),
        P(),
        P(),
        P(),
        P(None, None, "head"),
        P("head", None),
        P("head"),
        P("head"),
        P(None, PATCH, "head"),
    )
    return jax.shard_map(
        per_device,
        mesh=mesh,
        in_specs=placed,
        out_specs=(P((*PATCH, "head"), None), P(None, PATCH, "head")),
        check_vma=False,
    )
```

```python
import math

import jax
import jax.numpy as jnp
from jax import lax
from jax.experimental import pallas as pl
from jax.experimental.pallas import tpu as pltpu
from jax.sharding import PartitionSpec as P

HD = 128


def modulate(x_tokens, shift, scale_mod):
    values_f = x_tokens.astype(jnp.float32)
    center = jnp.mean(values_f, axis=-1, keepdims=True)
    spread = jnp.mean((values_f - center) * (values_f - center), axis=-1, keepdims=True)
    return ((values_f - center) * lax.rsqrt(spread + 1e-06) * (1.0 + scale_mod) + shift).astype(
        jnp.bfloat16
    )


def per_device(x_tokens, shift, scale_mod, gate, w_qkv, w_out, gain_q, gain_k, stale_kv):
    width = w_qkv.shape[1]
    raw, squares = _modulate_project(
        lax.all_gather(x_tokens, "head", axis=0, tiled=True), shift, scale_mod, w_qkv
    )
    squares = jnp.sum(lax.all_gather(squares, "head"), axis=0).T
    inverse = lax.rsqrt(squares / width + 1e-06)
    queries = (raw[0] * inverse[0][:, None] * gain_q).astype(jnp.bfloat16)
    keys = (raw[1] * inverse[1][:, None] * gain_k).astype(jnp.bfloat16)
    values = raw[2].astype(jnp.bfloat16)
    fresh_kv = jnp.stack([keys, values])
    parts = _exchange_attention(stale_kv, queries, keys, values)
    own_rows = x_tokens.shape[0]
    groups = queries.shape[0] // own_rows
    whole_terms = _combine_project(parts, w_out)
    pieces = lax.all_to_all(
        whole_terms.reshape(groups, own_rows, whole_terms.shape[1]), "head", 0, 0, tiled=True
    )
    projected = jnp.sum(pieces.astype(jnp.float32), axis=0)
    update = (projected * gate).astype(jnp.bfloat16)
    return (update, fresh_kv)


def _modulate_project_kernel(x_ref, shift_ref, scale_ref, w_ref, raw_ref, squares_ref):
    values_f = x_ref[...].astype(jnp.float32)
    center = jnp.mean(values_f, axis=-1, keepdims=True)
    spread = jnp.mean((values_f - center) * (values_f - center), axis=-1, keepdims=True)
    normed = (values_f - center) * lax.rsqrt(spread + 1e-06) * (1.0 + scale_ref[...]) + shift_ref[...]
    normed = normed.astype(jnp.bfloat16)
    lane = lax.broadcasted_iota(jnp.int32, (x_ref.shape[0], HD), 1)
    sums = jnp.zeros((x_ref.shape[0], HD), jnp.float32)
    for c in range(w_ref.shape[0]):
        raw = jnp.dot(normed, w_ref[c], preferred_element_type=jnp.float32)
        raw_ref[c] = raw
        if c < 2:
            sums = jnp.where(lane == c, jnp.sum(raw * raw, axis=1, keepdims=True), sums)
    squares_ref[...] = sums


def _modulate_project(x, shift, scale_mod, w_qkv):
    vmem = pl.BlockSpec(memory_space=pltpu.VMEM)
    rows = x.shape[0]
    raw, sums = pl.pallas_call(
        _modulate_project_kernel,
        out_shape=(
            jax.ShapeDtypeStruct((w_qkv.shape[0], rows, w_qkv.shape[2]), jnp.float32),
            jax.ShapeDtypeStruct((rows, HD), jnp.float32),
        ),
        in_specs=[vmem] * 4,
        out_specs=(vmem, vmem),
        compiler_params=pltpu.CompilerParams(vmem_limit_bytes=48 * 1024 * 1024),
    )(x, shift.reshape(1, -1), scale_mod.reshape(1, -1), w_qkv)
    return raw, sums[:, :2]


def _split_dot(weights, values, dims):
    high = weights.astype(jnp.bfloat16)
    low = (weights - high.astype(jnp.float32)).astype(jnp.bfloat16)
    out = lax.dot_general(high, values, dims, preferred_element_type=jnp.float32)
    return out + lax.dot_general(low, values, dims, preferred_element_type=jnp.float32)


def _partial_kernel(mask_ref, q_ref, k_ref, v_ref, kv_ref, out_ref):
    queries_n = q_ref.shape[0]
    slab = k_ref.shape[0]
    count = kv_ref.shape[1] // slab
    heads = q_ref.shape[1] // HD
    scale = math.sqrt(HD)
    is_own = mask_ref[...] > 0
    fresh_col = jnp.max(mask_ref[...], axis=0, keepdims=True) > 0
    contract_minor = (((1,), (1,)), ((), ()))
    contract_major = (((0,), (0,)), ((), ()))
    lane = lax.broadcasted_iota(jnp.int32, (queries_n, HD), 1)
    spread = jnp.zeros((queries_n, HD), jnp.float32)
    for h in range(heads):
        cols = pl.ds(h * HD, HD)
        query = q_ref[:, cols]
        scores = lax.dot_general(
            kv_ref[0, :, cols], query, contract_minor,
            preferred_element_type=jnp.float32,
        ) / scale
        scores = scores.reshape(count, slab, queries_n)
        block_max = jnp.max(scores, axis=1)
        expo = jnp.exp(scores - block_max[:, None, :])
        totals = jnp.sum(expo, axis=1)
        weights = expo.astype(jnp.bfloat16).astype(jnp.float32)
        fresh_scores = lax.dot_general(
            k_ref[:, cols], query, contract_minor, preferred_element_type=jnp.float32
        ) / scale
        fresh_max = jnp.max(fresh_scores, axis=0, keepdims=True)
        fresh_expo = jnp.exp(fresh_scores - fresh_max)
        fresh_total = jnp.sum(fresh_expo, axis=0, keepdims=True)
        fresh_weights = fresh_expo.astype(jnp.bfloat16).astype(jnp.float32)
        top = jnp.max(jnp.where(is_own, -jnp.inf, block_max), axis=0, keepdims=True)
        top = jnp.maximum(top, jnp.where(fresh_col, fresh_max, -jnp.inf))
        factor = jnp.where(is_own, 0.0, jnp.exp(block_max - top))
        fresh_factor = jnp.where(fresh_col, jnp.exp(fresh_max - top), 0.0)
        total = jnp.sum(factor * totals, axis=0, keepdims=True) + fresh_factor * fresh_total
        mixed = (factor[:, None, :] * weights).reshape(count * slab, queries_n)
        numer = _split_dot(mixed, kv_ref[1, :, cols], contract_major)
        numer = numer + _split_dot(fresh_factor * fresh_weights, v_ref[:, cols], contract_major)
        out_ref[:, cols] = (numer / total.reshape(queries_n, 1)).astype(out_ref.dtype)
        log_weight = (top + jnp.log(total)).reshape(queries_n, 1)
        spread = jnp.where(lane % 8 == h, log_weight, spread)
    high = spread.astype(jnp.bfloat16).astype(jnp.float32)
    middle = (spread - high).astype(jnp.bfloat16).astype(jnp.float32)
    low = spread - high - middle
    coded = jnp.where(lane < 8, high, jnp.where(lane < 16, middle, jnp.where(lane < 24, low, 0.0)))
    out_ref[:, pl.ds(heads * HD, HD)] = coded.astype(out_ref.dtype)


def _partial_attention(mask, group_queries, keys, values, near_kv):
    vmem = pl.BlockSpec(memory_space=pltpu.VMEM)
    rows, width = group_queries.shape
    return pl.pallas_call(
        _partial_kernel,
        out_shape=jax.ShapeDtypeStruct((rows, width + HD), jnp.bfloat16),
        in_specs=[vmem] * 5,
        out_specs=vmem,
        compiler_params=pltpu.CompilerParams(vmem_limit_bytes=48 * 1024 * 1024),
    )(mask, group_queries, keys, values, near_kv)


def _exchange_attention(stale_kv, queries, keys, values):
    slab, width = queries.shape
    kv_axes, q_axes = PATCH[-1:], PATCH[:-1]
    m = math.prod(lax.psum(1, name) for name in kv_axes)
    spread_kv = jnp.broadcast_to(stale_kv[:, None], (2, m) + stale_kv.shape[1:])
    near_kv = lax.all_to_all(spread_kv.reshape(2, m * slab, width), kv_axes, 1, 1, tiled=True)
    count = near_kv.shape[1] // slab
    n = math.prod(lax.psum(1, name) for name in q_axes)
    spread = jnp.broadcast_to(queries[None], (n, slab, width)).reshape(n * slab, width)
    group_queries = lax.all_to_all(spread, q_axes, 0, 0, tiled=True)
    block_ids = jnp.arange(count, dtype=jnp.int32)[:, None]
    slab_ids = (jnp.arange(n * slab, dtype=jnp.int32) // slab)[None, :]
    mask = (block_ids == lax.axis_index(kv_axes)) & (slab_ids == lax.axis_index(q_axes))
    partial = _partial_attention(mask.astype(jnp.int32), group_queries, keys, values, near_kv)
    return lax.all_to_all(partial.reshape(n, slab, width + HD), q_axes, 0, 0, tiled=True)


def _combine_kernel(parts_ref, w_ref, out_ref):
    n, slab, width = parts_ref.shape
    heads = width // HD - 1
    lane = lax.broadcasted_iota(jnp.int32, (slab, HD), 1)
    coded = [parts_ref[i, :, pl.ds(heads * HD, HD)].astype(jnp.float32) for i in range(n)]
    columns = []
    for h in range(heads):
        pick = (lane % 8 == h) & (lane < 24)
        log_weight = [jnp.sum(jnp.where(pick, c, 0.0), axis=1, keepdims=True) for c in coded]
        top = log_weight[0]
        for w in log_weight[1:]:
            top = jnp.maximum(top, w)
        factor = [jnp.exp(w - top) for w in log_weight]
        total = factor[0]
        for f in factor[1:]:
            total = total + f
        numer = jnp.zeros((slab, HD), jnp.float32)
        for i in range(n):
            numer = numer + factor[i] * parts_ref[i, :, pl.ds(h * HD, HD)].astype(jnp.float32)
        columns.append(numer / total)
    attn = jnp.concatenate(columns, axis=1).astype(jnp.bfloat16)
    out_ref[...] = jnp.dot(attn, w_ref[...], preferred_element_type=jnp.float32).astype(out_ref.dtype)


def _combine_project(parts, w_out):
    vmem = pl.BlockSpec(memory_space=pltpu.VMEM)
    return pl.pallas_call(
        _combine_kernel,
        out_shape=jax.ShapeDtypeStruct((parts.shape[1], w_out.shape[1]), jnp.bfloat16),
        in_specs=[vmem] * 2,
        out_specs=vmem,
    )(parts, w_out)


def _split_patch(mesh):
    patch = mesh.devices[:, 0]
    sizes = [len({d.coords[k] for d in patch}) for k in range(3)]
    sizes = [n for n in sizes if n > 1]
    if math.prod(sizes) != patch.shape[0] or len(sizes) < 2:
        return mesh, ("patch",)
    names = tuple(f"patch{k}" for k in range(len(sizes)))
    devices = mesh.devices.reshape(*sizes, mesh.devices.shape[1])
    return jax.sharding.Mesh(devices, names + ("head",)), names


PATCH = ("patch",)


def solution(mesh):
    global PATCH
    mesh, PATCH = _split_patch(mesh)
    placed = (
        P((*PATCH, "head"), None),
        P(),
        P(),
        P(),
        P(None, None, "head"),
        P("head", None),
        P("head"),
        P("head"),
        P(None, PATCH, "head"),
    )
    return jax.shard_map(
        per_device,
        mesh=mesh,
        in_specs=placed,
        out_specs=(P((*PATCH, "head"), None), P(None, PATCH, "head")),
        check_vma=False,
    )
```

```python
import math

import jax
import jax.numpy as jnp
from jax import lax
from jax.experimental import pallas as pl
from jax.experimental.pallas import tpu as pltpu
from jax.sharding import PartitionSpec as P

HD = 128


def modulate(x_tokens, shift, scale_mod):
    values_f = x_tokens.astype(jnp.float32)
    center = jnp.mean(values_f, axis=-1, keepdims=True)
    spread = jnp.mean((values_f - center) * (values_f - center), axis=-1, keepdims=True)
    return ((values_f - center) * lax.rsqrt(spread + 1e-06) * (1.0 + scale_mod) + shift).astype(
        jnp.bfloat16
    )


def per_device(x_tokens, shift, scale_mod, gate, w_qkv, w_out, gain_q, gain_k, stale_kv):
    width = w_qkv.shape[1]
    raw, squares = _modulate_project(
        lax.all_gather(x_tokens, "head", axis=0, tiled=True), shift, scale_mod, w_qkv
    )
    squares = jnp.sum(lax.all_gather(squares, "head"), axis=0).T
    inverse = lax.rsqrt(squares / width + 1e-06)
    queries = (raw[0] * inverse[0][:, None] * gain_q).astype(jnp.bfloat16)
    keys = (raw[1] * inverse[1][:, None] * gain_k).astype(jnp.bfloat16)
    values = raw[2].astype(jnp.bfloat16)
    fresh_kv = jnp.stack([keys, values])
    parts = _exchange_attention(stale_kv, queries, keys, values)
    own_rows = x_tokens.shape[0]
    groups = queries.shape[0] // own_rows
    whole_terms = _combine_project(parts, w_out)
    pieces = lax.all_to_all(
        whole_terms.reshape(groups, own_rows, whole_terms.shape[1]), "head", 0, 0, tiled=True
    )
    projected = jnp.sum(pieces.astype(jnp.float32), axis=0)
    update = (projected * gate).astype(jnp.bfloat16)
    return (update, fresh_kv)


def _modulate_project_kernel(x_ref, shift_ref, scale_ref, w_ref, raw_ref, squares_ref):
    values_f = x_ref[...].astype(jnp.float32)
    center = jnp.mean(values_f, axis=-1, keepdims=True)
    spread = jnp.mean((values_f - center) * (values_f - center), axis=-1, keepdims=True)
    normed = (values_f - center) * lax.rsqrt(spread + 1e-06) * (1.0 + scale_ref[...]) + shift_ref[...]
    normed = normed.astype(jnp.bfloat16)
    lane = lax.broadcasted_iota(jnp.int32, (x_ref.shape[0], HD), 1)
    sums = jnp.zeros((x_ref.shape[0], HD), jnp.float32)
    for c in range(w_ref.shape[0]):
        raw = jnp.dot(normed, w_ref[c], preferred_element_type=jnp.float32)
        raw_ref[c] = raw
        if c < 2:
            sums = jnp.where(lane == c, jnp.sum(raw * raw, axis=1, keepdims=True), sums)
    squares_ref[...] = sums


def _modulate_project(x, shift, scale_mod, w_qkv):
    vmem = pl.BlockSpec(memory_space=pltpu.VMEM)
    rows = x.shape[0]
    raw, sums = pl.pallas_call(
        _modulate_project_kernel,
        out_shape=(
            jax.ShapeDtypeStruct((w_qkv.shape[0], rows, w_qkv.shape[2]), jnp.float32),
            jax.ShapeDtypeStruct((rows, HD), jnp.float32),
        ),
        in_specs=[vmem] * 4,
        out_specs=(vmem, vmem),
        compiler_params=pltpu.CompilerParams(vmem_limit_bytes=48 * 1024 * 1024),
    )(x, shift.reshape(1, -1), scale_mod.reshape(1, -1), w_qkv)
    return raw, sums[:, :2]


def _split_dot(weights, values, dims):
    high = weights.astype(jnp.bfloat16)
    low = (weights - high.astype(jnp.float32)).astype(jnp.bfloat16)
    out = lax.dot_general(high, values, dims, preferred_element_type=jnp.float32)
    return out + lax.dot_general(low, values, dims, preferred_element_type=jnp.float32)


def _partial_kernel(mask_ref, q_ref, k_ref, v_ref, kv_ref, out_ref):
    queries_n = q_ref.shape[0]
    slab = k_ref.shape[0]
    count = kv_ref.shape[1] // slab
    heads = q_ref.shape[1] // HD
    scale = math.sqrt(HD)
    is_own = mask_ref[...] > 0
    fresh_col = jnp.max(mask_ref[...], axis=0, keepdims=True) > 0
    contract_minor = (((1,), (1,)), ((), ()))
    contract_major = (((0,), (0,)), ((), ()))
    lane = lax.broadcasted_iota(jnp.int32, (queries_n, HD), 1)
    spread = jnp.zeros((queries_n, HD), jnp.float32)
    for h in range(heads):
        cols = pl.ds(h * HD, HD)
        query = q_ref[:, cols]
        scores = lax.dot_general(
            kv_ref[0, :, cols], query, contract_minor,
            preferred_element_type=jnp.float32,
        ) / scale
        scores = scores.reshape(count, slab, queries_n)
        block_max = jnp.max(scores, axis=1)
        expo = jnp.exp(scores - block_max[:, None, :])
        totals = jnp.sum(expo, axis=1)
        weights = expo.astype(jnp.bfloat16).astype(jnp.float32)
        fresh_scores = lax.dot_general(
            k_ref[:, cols], query, contract_minor, preferred_element_type=jnp.float32
        ) / scale
        fresh_max = jnp.max(fresh_scores, axis=0, keepdims=True)
        fresh_expo = jnp.exp(fresh_scores - fresh_max)
        fresh_total = jnp.sum(fresh_expo, axis=0, keepdims=True)
        fresh_weights = fresh_expo.astype(jnp.bfloat16).astype(jnp.float32)
        top = jnp.max(jnp.where(is_own, -jnp.inf, block_max), axis=0, keepdims=True)
        top = jnp.maximum(top, jnp.where(fresh_col, fresh_max, -jnp.inf))
        factor = jnp.where(is_own, 0.0, jnp.exp(block_max - top))
        fresh_factor = jnp.where(fresh_col, jnp.exp(fresh_max - top), 0.0)
        total = jnp.sum(factor * totals, axis=0, keepdims=True) + fresh_factor * fresh_total
        mixed = (factor[:, None, :] * weights).reshape(count * slab, queries_n)
        numer = _split_dot(mixed, kv_ref[1, :, cols], contract_major)
        numer = numer + _split_dot(fresh_factor * fresh_weights, v_ref[:, cols], contract_major)
        out_ref[:, cols] = (numer / total.reshape(queries_n, 1)).astype(out_ref.dtype)
        log_weight = (top + jnp.log(total)).reshape(queries_n, 1)
        spread = jnp.where(lane % 8 == h, log_weight, spread)
    high = spread.astype(jnp.bfloat16).astype(jnp.float32)
    middle = (spread - high).astype(jnp.bfloat16).astype(jnp.float32)
    low = spread - high - middle
    coded = jnp.where(lane < 8, high, jnp.where(lane < 16, middle, jnp.where(lane < 24, low, 0.0)))
    out_ref[:, pl.ds(heads * HD, HD)] = coded.astype(out_ref.dtype)


def _partial_attention(mask, group_queries, keys, values, near_kv):
    vmem = pl.BlockSpec(memory_space=pltpu.VMEM)
    rows, width = group_queries.shape
    return pl.pallas_call(
        _partial_kernel,
        out_shape=jax.ShapeDtypeStruct((rows, width + HD), jnp.bfloat16),
        in_specs=[vmem] * 5,
        out_specs=vmem,
        compiler_params=pltpu.CompilerParams(vmem_limit_bytes=48 * 1024 * 1024),
    )(mask, group_queries, keys, values, near_kv)


def _exchange_attention(stale_kv, queries, keys, values):
    slab, width = queries.shape
    kv_axes, q_axes = PATCH[-1:], PATCH[:-1]
    m = math.prod(lax.psum(1, name) for name in kv_axes)
    spread_kv = jnp.broadcast_to(stale_kv[:, None], (2, m) + stale_kv.shape[1:])
    near_kv = lax.all_to_all(spread_kv.reshape(2, m * slab, width), kv_axes, 1, 1, tiled=True)
    count = near_kv.shape[1] // slab
    n = math.prod(lax.psum(1, name) for name in q_axes)
    spread = jnp.broadcast_to(queries[None], (n, slab, width)).reshape(n * slab, width)
    group_queries = lax.all_to_all(spread, q_axes, 0, 0, tiled=True)
    block_ids = jnp.arange(count, dtype=jnp.int32)[:, None]
    slab_ids = (jnp.arange(n * slab, dtype=jnp.int32) // slab)[None, :]
    mask = (block_ids == lax.axis_index(kv_axes)) & (slab_ids == lax.axis_index(q_axes))
    partial = _partial_attention(mask.astype(jnp.int32), group_queries, keys, values, near_kv)
    return lax.all_to_all(partial.reshape(n, slab, width + HD), q_axes, 0, 0, tiled=True)


def _combine_kernel(parts_ref, w_ref, out_ref):
    n, slab, width = parts_ref.shape
    heads = width // HD - 1
    row = lax.broadcasted_iota(jnp.int32, (HD, HD), 0)
    coded = [parts_ref[i, :, pl.ds(heads * HD, HD)] for i in range(n)]
    columns = []
    for h in range(heads):
        pick = ((row % 8 == h) & (row < 24)).astype(jnp.bfloat16)
        log_weight = [jnp.dot(c, pick, preferred_element_type=jnp.float32) for c in coded]
        top = log_weight[0]
        for w in log_weight[1:]:
            top = jnp.maximum(top, w)
        factor = [jnp.exp(w - top) for w in log_weight]
        total = factor[0]
        for f in factor[1:]:
            total = total + f
        numer = jnp.zeros((slab, HD), jnp.float32)
        for i in range(n):
            numer = numer + factor[i] * parts_ref[i, :, pl.ds(h * HD, HD)].astype(jnp.float32)
        columns.append(numer / total)
    attn = jnp.concatenate(columns, axis=1).astype(jnp.bfloat16)
    out_ref[...] = jnp.dot(attn, w_ref[...], preferred_element_type=jnp.float32).astype(out_ref.dtype)


def _combine_project(parts, w_out):
    vmem = pl.BlockSpec(memory_space=pltpu.VMEM)
    return pl.pallas_call(
        _combine_kernel,
        out_shape=jax.ShapeDtypeStruct((parts.shape[1], w_out.shape[1]), jnp.bfloat16),
        in_specs=[vmem] * 2,
        out_specs=vmem,
    )(parts, w_out)


def _split_patch(mesh):
    patch = mesh.devices[:, 0]
    sizes = [len({d.coords[k] for d in patch}) for k in range(3)]
    sizes = [n for n in sizes if n > 1]
    if math.prod(sizes) != patch.shape[0] or len(sizes) < 2:
        return mesh, ("patch",)
    names = tuple(f"patch{k}" for k in range(len(sizes)))
    devices = mesh.devices.reshape(*sizes, mesh.devices.shape[1])
    return jax.sharding.Mesh(devices, names + ("head",)), names


PATCH = ("patch",)


def solution(mesh):
    global PATCH
    mesh, PATCH = _split_patch(mesh)
    placed = (
        P((*PATCH, "head"), None),
        P(),
        P(),
        P(),
        P(None, None, "head"),
        P("head", None),
        P("head"),
        P("head"),
        P(None, PATCH, "head"),
    )
    return jax.shard_map(
        per_device,
        mesh=mesh,
        in_specs=placed,
        out_specs=(P((*PATCH, "head"), None), P(None, PATCH, "head")),
        check_vma=False,
    )
```
